256 devices in a mesh: ctx: 16 (over z, core), tp: 16 (over x, y).
Axes of the slice: x: 4, y: 4, z: 8, core: 2. Of those that a mesh axis runs over, the one named last changes fastest.
Arguments:
- q_act: bfloat16 [64, 128, 4096], P('ctx', None, 'tp'), may hold values from -16 to 16
- k_act: bfloat16 [64, 128, 4096], P('ctx', None, 'tp'), may hold values from -16 to 16
- v_act: bfloat16 [64, 128, 4096], P('ctx', None, 'tp'), may hold values from -6 to 6
- grad_out: bfloat16 [8192, 4096], P(('ctx', 'tp')), may hold values from -24 to 24
- w_out: bfloat16 [4096, 4096], P(None, 'tp'), may hold values from -0.09375 to 0.09375
- nbr_tiles: int32 [64, 12], replicated, may hold values from 0 to 63, as said below
- nbr_valid: int32 [64, 12], replicated, may hold values from 0 to 1, as said below
- slot_of: int32 [64], replicated, may hold values from 0 to 63, as said below
Outputs:
- grad_q: bfloat16 [64, 128, 4096], P('ctx', None, 'tp')
- grad_k: bfloat16 [64, 128, 4096], P('ctx', None, 'tp')
- grad_v: bfloat16 [64, 128, 4096], P('ctx', None, 'tp')
- grad_w_out: bfloat16 [4096, 4096], P('ctx', 'tp')
The draws below stay inside these ranges and needn't reach their ends.
Inputs may be any that keep to these rules, and one draw needn't show every extreme that they name: `nbr_tiles`: row t lists scenario tiles linked to tile t; the live entries of a row name distinct tiles, one of them t itself. `nbr_valid`: every row has at least one live entry; a tile is named by live entries of at most 12 rows. `slot_of`: a permutation; slots c * 4 to c * 4 + 3 are held by index c of ctx.
All inputs are finite; a program needn't handle non-finite values.
Results may differ from the reference program's by a relative error of at most 0.024.
Values may be sent and summed in bfloat16 or wider, within the bound.
No kernel may reach another device: no remote copies, remote signals or barrier semaphores. Data moves between devices by JAX's collectives and lax.ppermute only.
A program may use at most 128 MiB of HBM per device.

```python
import math
import jax
import jax.numpy as jnp
from jax import lax

D = 4096
H = 32
HD = 128
TILE = 128
NBR = 12
TILES = 64
TOKENS = 8192


def query_key_pair(key):
    base = jax.random.fold_in(key, 7)
    key_query, key_keys = jax.random.split(base, 2)
    shape = (TILES, TILE, H * HD)
    query = jnp.clip(jax.random.normal(key_query, shape, jnp.float32), -6.0, 6.0)
    keys = jnp.clip(jax.random.normal(key_keys, shape, jnp.float32), -6.0, 6.0)
    return (query, keys)


def draw_q_act(key, part):
    query, keys = query_key_pair(key)
    return query.astype(jnp.bfloat16)


def draw_k_act(key, part):
    query, keys = query_key_pair(key)
    return keys.astype(jnp.bfloat16)


def slot_table(key):
    base = jax.random.fold_in(key, 23)
    return jax.random.permutation(base, TILES).astype(jnp.int32)


def draw_slot_of(key, part):
    return slot_table(key)


def neighbour_table(key):
    base = jax.random.fold_in(key, 11)
    key_perm, key_shift, key_live, key_hub, key_order = jax.random.split(base, 5)
    tile_ids = jnp.arange(TILES, dtype=jnp.int32)
    relabel = jax.random.permutation(key_perm, TILES).astype(jnp.int32)
    inverse = jnp.zeros((TILES,), jnp.int32).at[relabel].set(tile_ids)
    others = (jax.random.permutation(key_shift, TILES - 1) + 1).astype(jnp.int32)
    shifts = jnp.concatenate([jnp.zeros((1,), jnp.int32), others]).astype(jnp.int32)
    entry = jnp.arange(NBR, dtype=jnp.int32)
    offsets = shifts[entry % TILES]
    within = (entry < TILES).astype(jnp.int32)
    listed = inverse[(relabel[:, None] + offsets[None, :]) % TILES].astype(jnp.int32)
    chance = (jax.random.randint(key_live, (TILES, NBR), 0, 20, dtype=jnp.int32) < 11).astype(jnp.int32)
    usable = chance * within[None, :]
    usable = usable.at[:, 0].set(1)
    hub_pair = jax.random.randint(key_hub, (2,), 0, TILES, dtype=jnp.int32)
    hub_rows = inverse[(relabel[hub_pair[0]] - offsets) % TILES]
    usable = usable.at[hub_rows, entry].max(within)
    usable = usable.at[hub_pair[1]].max(within)
    usable = usable.astype(jnp.int32)
    ranks = jax.random.randint(key_order, (TILES, NBR), 0, 1 << 20, dtype=jnp.int32) * NBR + entry[None, :]
    placing = jnp.argsort(ranks, axis=1)
    return (jnp.take_along_axis(listed, placing, axis=1), jnp.take_along_axis(usable, placing, axis=1))


def draw_nbr_tiles(key, part):
    listed, usable = neighbour_table(key)
    return listed


def draw_nbr_valid(key, part):
    listed, usable = neighbour_table(key)
    return usable


def with_spikes(drawn, key, source, target, parts, factor):
    owner, partner = [(jnp.arange(drawn.shape[position]) // (drawn.shape[position] // parts)).reshape([-1 if axis == position else 1 for axis in range(drawn.ndim)]) for position in (source, target)]
    chosen = jax.random.permutation(key, parts)[partner]
    strong = (owner == chosen) | (owner == (partner + parts // 2) % parts)
    return jnp.where(strong, factor * drawn, drawn)


def block_levels(stream_key, shape, pieces, least, high):
    def one(position, shards_of):
        steps = jax.random.uniform(jax.random.fold_in(jax.random.fold_in(stream_key, 6), position), (shards_of,), jnp.float32, least / len(pieces), high / len(pieces))
        return jnp.repeat(jnp.exp(steps), shape[position] // shards_of).reshape((-1,) + (1,) * (len(shape) - position - 1))

    loudness = one(*pieces[0])
    for cut in pieces[1:]:
        loudness = loudness * one(*cut)
    return loudness


def normal_values(key, shape, deviation, bound, cuts=(), held_as=jnp.bfloat16):
    result = deviation * jax.random.normal(key, shape, jnp.float32)
    if cuts:
        result = result * block_levels(key, shape, cuts, -0.22, 0.18)
    return jnp.clip(result, -bound, bound).astype(held_as)


def bell_draw_with(stream_key, dims, width, most, shards, heavy, held_as=jnp.bfloat16):
    result = width * jax.random.normal(stream_key, dims, jnp.float32)
    if shards:
        result = result * block_levels(stream_key, dims, shards, -0.22, 0.18)
    return jnp.clip(with_spikes(result, jax.random.fold_in(stream_key, 3), *heavy), -most, most).astype(held_as)


def setup_inputs(seed: int = 0) -> dict:
    splits = jax.random.split(jax.random.key(seed), 9)
    q_act = draw_q_act(jax.random.fold_in(splits[8], 71), 0)
    k_act = draw_k_act(jax.random.fold_in(splits[8], 71), 0)
    v_act = normal_values(splits[2], (TILES, TILE, H * HD), 1.0, 6.0, ((0, 16), (2, 16)))
    grad_out = bell_draw_with(splits[3], (TOKENS, D), 1.0, 24.0, ((0, 256),), (0, 1, 256, 6.0))
    w_out = normal_values(splits[4], (D, H * HD), (H * HD) ** -0.5, 0.09375, ((1, 16),))
    nbr_tiles = draw_nbr_tiles(jax.random.fold_in(splits[8], 71), 0)
    nbr_valid = draw_nbr_valid(jax.random.fold_in(splits[8], 71), 0)
    slot_of = draw_slot_of(jax.random.fold_in(splits[8], 71), 0)
    return dict(q_act=q_act, k_act=k_act, v_act=v_act, grad_out=grad_out, w_out=w_out, nbr_tiles=nbr_tiles, nbr_valid=nbr_valid, slot_of=slot_of)


def slot_maps(nbr_tiles, nbr_valid, slot_of):
    slot_index = jnp.arange(TILES, dtype=jnp.int32)
    tile_at = jnp.zeros((TILES,), jnp.int32).at[slot_of].set(slot_index)
    key_slot = slot_of[nbr_tiles[tile_at]].astype(jnp.int32)
    live_mask = nbr_valid[tile_at].astype(jnp.int32)
    return (key_slot, live_mask)

def reference(q_act, k_act, v_act, grad_out, w_out, nbr_tiles, nbr_valid, slot_of):
    score_scale = 1.0 / math.sqrt(HD)
    key_slot, live_mask = slot_maps(nbr_tiles, nbr_valid, slot_of)
    grad_attn = jnp.dot(grad_out, w_out, preferred_element_type=jnp.float32).astype(jnp.bfloat16)
    grad_attn = grad_attn.reshape(TILES, TILE, H, HD)
    query_grid = q_act.reshape(TILES, TILE, H, HD)
    key_grid = k_act.reshape(TILES, TILE, H, HD)
    value_grid = v_act.reshape(TILES, TILE, H, HD)

    def one_tile(carry, slot):
        key_totals, value_totals = carry
        near_slots = key_slot[slot]
        live_cells = (live_mask[slot] > 0)[None, None, :, None]
        query_tile = query_grid[slot].astype(jnp.float32)
        near_keys = key_grid[near_slots].astype(jnp.float32)
        near_values = value_grid[near_slots].astype(jnp.float32)
        grad_tile = grad_attn[slot].astype(jnp.float32)
        scores = jnp.einsum('ahd,jbhd->hajb', query_tile, near_keys) * score_scale
        row_peak = lax.optimization_barrier(jnp.max(jnp.where(live_cells, scores, -1e+30), axis=(2, 3), keepdims=True))
        row_total = lax.optimization_barrier(jnp.sum(jnp.where(live_cells, jnp.exp(scores - row_peak), 0.0), axis=(2, 3), keepdims=True))
        log_total = row_peak + jnp.log(row_total)
        prob_full = jnp.where(live_cells, jnp.exp(scores - log_total), 0.0)
        prob_half = prob_full.astype(jnp.bfloat16)
        attn_tile = jnp.einsum('hajb,jbhd->ahd', prob_half.astype(jnp.float32), near_values).astype(jnp.bfloat16)
        row_delta = jnp.einsum('ahd,ahd->ha', grad_tile, attn_tile.astype(jnp.float32))[:, :, None, None]
        grad_prob = jnp.einsum('ahd,jbhd->hajb', grad_tile, near_values)
        grad_score = (prob_full * (grad_prob - row_delta)).astype(jnp.bfloat16)
        grad_query = jnp.einsum('hajb,jbhd->ahd', grad_score.astype(jnp.float32), near_keys) * score_scale
        key_terms = jnp.einsum('hajb,ahd->jbhd', grad_score.astype(jnp.float32), query_tile) * score_scale
        value_terms = jnp.einsum('hajb,ahd->jbhd', prob_half.astype(jnp.float32), grad_tile)
        live_weight = (live_mask[slot] > 0).astype(jnp.float32)[:, None, None, None]
        key_totals = key_totals.at[near_slots].add(key_terms * live_weight)
        value_totals = value_totals.at[near_slots].add(value_terms * live_weight)
        return ((key_totals, value_totals), (grad_query.astype(jnp.bfloat16), attn_tile))
    empty = jnp.zeros((TILES, TILE, H, HD), jnp.float32)
    (key_totals, value_totals), (grad_query, attn_out) = lax.scan(one_tile, (empty, empty), jnp.arange(TILES, dtype=jnp.int32))
    attn_flat = attn_out.reshape(TOKENS, H * HD)
    grad_weight = jnp.dot(grad_out.T, attn_flat, preferred_element_type=jnp.float32).astype(jnp.bfloat16)
    grad_q = grad_query.reshape(TILES, TILE, H * HD)
    grad_k = key_totals.astype(jnp.bfloat16).reshape(TILES, TILE, H * HD)
    grad_v = value_totals.astype(jnp.bfloat16).reshape(TILES, TILE, H * HD)
    return (grad_q, grad_k, grad_v, grad_weight)
```

```python
import math

import jax
import jax.numpy as jnp
from jax import lax
from jax.sharding import Mesh
from jax.sharding import PartitionSpec as P

HD = 128
CORES = 2


def slot_tables(nbr_tiles, nbr_valid, slot_of):
    tile_count = slot_of.shape[0]
    slot_index = jnp.arange(tile_count, dtype=jnp.int32)
    matches = (slot_of[:, None] == slot_index[None, :]).astype(jnp.int32)
    near_tiles = jnp.einsum("ts,tj->sj", matches, nbr_tiles)
    live_mask = jnp.einsum("ts,tj->sj", matches, nbr_valid)
    found = (near_tiles[:, :, None] == slot_index[None, None, :]).astype(jnp.int32)
    key_slot = jnp.sum(found * slot_of[None, None, :], axis=2)
    return (key_slot, live_mask)


def to_head(arrays, local_tiles, tile_len, heads_here):
    stacked = jnp.stack(
        [a.reshape(local_tiles, tile_len, heads_here, HD) for a in arrays], axis=1
    )
    moved = lax.all_to_all(stacked, "core", split_axis=3, concat_axis=0, tiled=True)
    return moved.reshape(local_tiles * heads_here, len(arrays), tile_len, HD)


def from_head(arrays, local_tiles, tile_len, heads_here):
    stacked = jnp.stack(arrays, axis=1)[:, :, :, None, :]
    moved = lax.all_to_all(stacked, "core", split_axis=0, concat_axis=3, tiled=True)
    return tuple(
        moved[:, n].reshape(local_tiles, tile_len, heads_here * HD) for n in range(len(arrays))
    )


def per_device(q_act, k_act, v_act, grad_out, w_out, nbr_tiles, nbr_valid, slot_of):
    local_tiles, tile_len, col_width = q_act.shape
    heads_here = col_width // HD
    score_scale = 1.0 / math.sqrt(HD)
    chip_tiles = local_tiles * heads_here
    first_slot = lax.axis_index("z") * chip_tiles
    key_slot, live_mask = slot_tables(nbr_tiles, nbr_valid, slot_of)
    tile_count = key_slot.shape[0]
    list_len = key_slot.shape[1]
    near_slots = lax.dynamic_slice_in_dim(key_slot, first_slot, chip_tiles, 0)
    near_live = lax.dynamic_slice_in_dim(live_mask, first_slot, chip_tiles, 0)

    full_rows = lax.all_gather(grad_out, "tp", axis=0, tiled=True)
    grad_flat = jnp.dot(full_rows, w_out, preferred_element_type=jnp.float32).astype(jnp.bfloat16)
    grad_tiles = grad_flat.reshape(local_tiles, tile_len, col_width)

    head_parts = to_head((q_act, k_act, v_act, grad_tiles), local_tiles, tile_len, heads_here)
    query_h = head_parts[:, 0]
    key_h = head_parts[:, 1]
    value_h = head_parts[:, 2]
    grad_h = head_parts[:, 3]

    kv_all = lax.all_gather(head_parts[:, 1:3], "z", axis=0, tiled=True)
    near = kv_all[near_slots.reshape(-1)].reshape(chip_tiles, list_len, 2, tile_len, HD)
    near_keys = near[:, :, 0].reshape(chip_tiles, list_len * tile_len, HD)
    near_values = near[:, :, 1].reshape(chip_tiles, list_len * tile_len, HD)
    live_cells = jnp.repeat(near_live > 0, tile_len, axis=1)[:, None, :]

    scores = (
        jnp.einsum("sad,sbd->sab", query_h, near_keys, preferred_element_type=jnp.float32)
        * score_scale
    )
    row_peak = jnp.max(jnp.where(live_cells, scores, -1e30), axis=2, keepdims=True)
    row_total = jnp.sum(
        jnp.where(live_cells, jnp.exp(scores - row_peak), 0.0), axis=2, keepdims=True
    )
    log_total = row_peak + jnp.log(row_total)
    prob_full = jnp.where(live_cells, jnp.exp(scores - log_total), 0.0)
    prob_half = prob_full.astype(jnp.bfloat16)
    attn_h = jnp.einsum(
        "sab,sbd->sad", prob_half, near_values, preferred_element_type=jnp.float32
    ).astype(jnp.bfloat16)
    row_delta = jnp.einsum("sad,sad->sa", grad_h, attn_h, preferred_element_type=jnp.float32)
    grad_prob = jnp.einsum(
        "sad,sbd->sab", grad_h, near_values, preferred_element_type=jnp.float32
    )
    grad_score = (prob_full * (grad_prob - row_delta[:, :, None])).astype(jnp.bfloat16)
    grad_query_h = (
        jnp.einsum("sab,sbd->sad", grad_score, near_keys, preferred_element_type=jnp.float32)
        * score_scale
    ).astype(jnp.bfloat16)

    attn_tiles, grad_q = from_head((attn_h, grad_query_h), local_tiles, tile_len, heads_here)

    qg_all = lax.all_gather(
        jnp.stack([query_h, grad_h], axis=1), "z", axis=0, tiled=True
    )
    stats_all = lax.all_gather(
        jnp.stack([log_total[:, :, 0], row_delta], axis=1), "z", axis=0, tiled=True
    )

    owned_slots = first_slot + jnp.arange(chip_tiles, dtype=jnp.int32)
    pair_hits = (key_slot[:, :, None] == owned_slots[None, None, :]) & (live_mask[:, :, None] > 0)
    named_by = jnp.any(pair_hits, axis=1).astype(jnp.int32)
    rank_of = jnp.cumsum(named_by, axis=0) - 1
    list_pos = jnp.arange(list_len, dtype=jnp.int32)
    placed = (named_by[:, :, None] > 0) & (rank_of[:, :, None] == list_pos[None, None, :])
    slot_index = jnp.arange(tile_count, dtype=jnp.int32)
    picked = jnp.sum(placed.astype(jnp.int32) * slot_index[:, None, None], axis=0)
    picked_live = jnp.any(placed, axis=0)

    rows = qg_all[picked.reshape(-1)].reshape(chip_tiles, list_len, 2, tile_len, HD)
    query_rows = rows[:, :, 0].reshape(chip_tiles, list_len * tile_len, HD)
    grad_rows = rows[:, :, 1].reshape(chip_tiles, list_len * tile_len, HD)
    stat_rows = stats_all[picked.reshape(-1)].reshape(chip_tiles, list_len, 2, tile_len)
    total_rows = stat_rows[:, :, 0].reshape(chip_tiles, 1, list_len * tile_len)
    delta_rows = stat_rows[:, :, 1].reshape(chip_tiles, 1, list_len * tile_len)
    keep_pair = jnp.repeat(picked_live, tile_len, axis=1)[:, None, :]

    owner_scores = (
        jnp.einsum("tbd,tad->tba", key_h, query_rows, preferred_element_type=jnp.float32)
        * score_scale
    )
    owner_probs = jnp.where(keep_pair, jnp.exp(owner_scores - total_rows), 0.0)
    owner_grad_prob = jnp.einsum(
        "tbd,tad->tba", value_h, grad_rows, preferred_element_type=jnp.float32
    )
    owner_grad_score = (owner_probs * (owner_grad_prob - delta_rows)).astype(jnp.bfloat16)
    grad_key_h = (
        jnp.einsum("tba,tad->tbd", owner_grad_score, query_rows, preferred_element_type=jnp.float32)
        * score_scale
    ).astype(jnp.bfloat16)
    grad_value_h = jnp.einsum(
        "tba,tad->tbd", owner_probs.astype(jnp.bfloat16), grad_rows, preferred_element_type=jnp.float32
    ).astype(jnp.bfloat16)

    grad_k, grad_v = from_head((grad_key_h, grad_value_h), local_tiles, tile_len, heads_here)

    attn_flat = attn_tiles.reshape(local_tiles * tile_len, col_width)
    grad_weight = lax.psum_scatter(
        lax.dot_general(
            full_rows, attn_flat, (((0,), (0,)), ((), ())), preferred_element_type=jnp.float32
        ).astype(jnp.bfloat16),
        ("z", "core"),
        scatter_dimension=0,
        tiled=True,
    )
    return (grad_q, grad_k, grad_v, grad_weight)


def solution(mesh):
    ctx_count = mesh.shape["ctx"]
    tp_count = mesh.shape["tp"]
    devices = mesh.devices.reshape(ctx_count // CORES, CORES, tp_count)
    chip_mesh = Mesh(devices, ("z", "core", "tp"))
    tiles = ("z", "core")
    in_specs = (
        P(tiles, None, "tp"),
        P(tiles, None, "tp"),
        P(tiles, None, "tp"),
        P((*tiles, "tp"), None),
        P(None, "tp"),
        P(),
        P(),
        P(),
    )
    out_specs = (
        P(tiles, None, "tp"),
        P(tiles, None, "tp"),
        P(tiles, None, "tp"),
        P(tiles, "tp"),
    )
    return jax.shard_map(
        per_device, mesh=chip_mesh, in_specs=in_specs, out_specs=out_specs, check_vma=False
    )
```

```python
import math

import jax
import jax.numpy as jnp
from jax import lax
from jax.sharding import Mesh
from jax.sharding import PartitionSpec as P

HD = 128
CORES = 2


def slot_tables(nbr_tiles, nbr_valid, slot_of):
    tile_count = slot_of.shape[0]
    slot_index = jnp.arange(tile_count, dtype=jnp.int32)
    matches = (slot_of[:, None] == slot_index[None, :]).astype(jnp.int32)
    near_tiles = jnp.einsum("ts,tj->sj", matches, nbr_tiles)
    live_mask = jnp.einsum("ts,tj->sj", matches, nbr_valid)
    found = (near_tiles[:, :, None] == slot_index[None, None, :]).astype(jnp.int32)
    key_slot = jnp.sum(found * slot_of[None, None, :], axis=2)
    return (key_slot, live_mask)


def to_head(arrays, local_tiles, tile_len, heads_here):
    stacked = jnp.stack(
        [a.reshape(local_tiles, tile_len, heads_here, HD) for a in arrays], axis=1
    )
    moved = lax.all_to_all(stacked, "core", split_axis=3, concat_axis=0, tiled=True)
    return moved.reshape(local_tiles * heads_here, len(arrays), tile_len, HD)


def from_head(arrays, local_tiles, tile_len, heads_here):
    stacked = jnp.stack(arrays, axis=1)[:, :, :, None, :]
    moved = lax.all_to_all(stacked, "core", split_axis=0, concat_axis=3, tiled=True)
    return tuple(
        moved[:, n].reshape(local_tiles, tile_len, heads_here * HD) for n in range(len(arrays))
    )


def ring_gather(x, axis, count):
    ahead = [(i, (i - 1) % count) for i in range(count)]
    behind = [(i, (i + 1) % count) for i in range(count)]
    half = count // 2
    later = [x]
    earlier = []
    down = x
    up = x
    for _ in range(1, half):
        down = lax.ppermute(down, axis, ahead)
        up = lax.ppermute(up, axis, behind)
        later.append(down)
        earlier.append(up)
    if count % 2 == 0 and count > 1:
        cut = x.shape[0] // 2
        first = lax.ppermute(up[:cut], axis, behind)
        second = lax.ppermute(down[cut:], axis, ahead)
        later.append(jnp.concatenate([first, second], axis=0))
    return jnp.concatenate(later + earlier[::-1], axis=0)


def ring_index(slots, own, chip_tiles, count):
    return ((slots // chip_tiles - own) % count) * chip_tiles + slots % chip_tiles


def per_device(q_act, k_act, v_act, grad_out, w_out, nbr_tiles, nbr_valid, slot_of):
    local_tiles, tile_len, col_width = q_act.shape
    heads_here = col_width // HD
    score_scale = 1.0 / math.sqrt(HD)
    chip_tiles = local_tiles * heads_here
    z_count = lax.axis_size("z")
    own_z = lax.axis_index("z")
    first_slot = own_z * chip_tiles
    key_slot, live_mask = slot_tables(nbr_tiles, nbr_valid, slot_of)
    tile_count = key_slot.shape[0]
    list_len = key_slot.shape[1]
    near_slots = lax.dynamic_slice_in_dim(key_slot, first_slot, chip_tiles, 0)
    near_live = lax.dynamic_slice_in_dim(live_mask, first_slot, chip_tiles, 0)

    full_rows = lax.all_gather(grad_out, "tp", axis=0, tiled=True)
    grad_flat = jnp.dot(full_rows, w_out, preferred_element_type=jnp.float32).astype(jnp.bfloat16)
    grad_tiles = grad_flat.reshape(local_tiles, tile_len, col_width)

    head_parts = to_head((k_act, v_act, q_act), local_tiles, tile_len, heads_here)
    key_h = head_parts[:, 0]
    value_h = head_parts[:, 1]
    query_h = head_parts[:, 2]
    grad_h = to_head((grad_tiles,), local_tiles, tile_len, heads_here)[:, 0]

    kv_all = ring_gather(head_parts[:, 0:2], "z", z_count)
    near_index = ring_index(near_slots.reshape(-1), own_z, chip_tiles, z_count)
    near = kv_all[near_index].reshape(chip_tiles, list_len, 2, tile_len, HD)
    near_keys = near[:, :, 0].reshape(chip_tiles, list_len * tile_len, HD)
    near_values = near[:, :, 1].reshape(chip_tiles, list_len * tile_len, HD)
    live_cells = jnp.repeat(near_live > 0, tile_len, axis=1)[:, None, :]

    scores = (
        jnp.einsum("sad,sbd->sab", query_h, near_keys, preferred_element_type=jnp.float32)
        * score_scale
    )
    row_peak = jnp.max(jnp.where(live_cells, scores, -1e30), axis=2, keepdims=True)
    row_total = jnp.sum(
        jnp.where(live_cells, jnp.exp(scores - row_peak), 0.0), axis=2, keepdims=True
    )
    log_total = row_peak + jnp.log(row_total)
    prob_full = jnp.where(live_cells, jnp.exp(scores - log_total), 0.0)
    prob_half = prob_full.astype(jnp.bfloat16)
    attn_h = jnp.einsum(
        "sab,sbd->sad", prob_half, near_values, preferred_element_type=jnp.float32
    ).astype(jnp.bfloat16)
    row_delta = jnp.einsum("sad,sad->sa", grad_h, attn_h, preferred_element_type=jnp.float32)
    grad_prob = jnp.einsum(
        "sad,sbd->sab", grad_h, near_values, preferred_element_type=jnp.float32
    )
    grad_score = (prob_full * (grad_prob - row_delta[:, :, None])).astype(jnp.bfloat16)
    grad_query_h = (
        jnp.einsum("sab,sbd->sad", grad_score, near_keys, preferred_element_type=jnp.float32)
        * score_scale
    ).astype(jnp.bfloat16)

    attn_tiles, grad_q = from_head((attn_h, grad_query_h), local_tiles, tile_len, heads_here)

    qg_all = ring_gather(jnp.stack([query_h, grad_h], axis=1), "z", z_count)
    stats_all = ring_gather(jnp.stack([log_total[:, :, 0], row_delta], axis=1), "z", z_count)

    owned_slots = first_slot + jnp.arange(chip_tiles, dtype=jnp.int32)
    pair_hits = (key_slot[:, :, None] == owned_slots[None, None, :]) & (live_mask[:, :, None] > 0)
    named_by = jnp.any(pair_hits, axis=1).astype(jnp.int32)
    rank_of = jnp.cumsum(named_by, axis=0) - 1
    list_pos = jnp.arange(list_len, dtype=jnp.int32)
    placed = (named_by[:, :, None] > 0) & (rank_of[:, :, None] == list_pos[None, None, :])
    slot_index = jnp.arange(tile_count, dtype=jnp.int32)
    picked = jnp.sum(placed.astype(jnp.int32) * slot_index[:, None, None], axis=0)
    picked_live = jnp.any(placed, axis=0)

    picked_index = ring_index(picked.reshape(-1), own_z, chip_tiles, z_count)
    rows = qg_all[picked_index].reshape(chip_tiles, list_len, 2, tile_len, HD)
    query_rows = rows[:, :, 0].reshape(chip_tiles, list_len * tile_len, HD)
    grad_rows = rows[:, :, 1].reshape(chip_tiles, list_len * tile_len, HD)
    stat_rows = stats_all[picked_index].reshape(chip_tiles, list_len, 2, tile_len)
    total_rows = stat_rows[:, :, 0].reshape(chip_tiles, 1, list_len * tile_len)
    delta_rows = stat_rows[:, :, 1].reshape(chip_tiles, 1, list_len * tile_len)
    keep_pair = jnp.repeat(picked_live, tile_len, axis=1)[:, None, :]

    owner_scores = (
        jnp.einsum("tbd,tad->tba", key_h, query_rows, preferred_element_type=jnp.float32)
        * score_scale
    )
    owner_probs = jnp.where(keep_pair, jnp.exp(owner_scores - total_rows), 0.0)
    owner_grad_prob = jnp.einsum(
        "tbd,tad->tba", value_h, grad_rows, preferred_element_type=jnp.float32
    )
    owner_grad_score = (owner_probs * (owner_grad_prob - delta_rows)).astype(jnp.bfloat16)
    grad_key_h = (
        jnp.einsum("tba,tad->tbd", owner_grad_score, query_rows, preferred_element_type=jnp.float32)
        * score_scale
    ).astype(jnp.bfloat16)
    grad_value_h = jnp.einsum(
        "tba,tad->tbd", owner_probs.astype(jnp.bfloat16), grad_rows, preferred_element_type=jnp.float32
    ).astype(jnp.bfloat16)

    grad_k, grad_v = from_head((grad_key_h, grad_value_h), local_tiles, tile_len, heads_here)

    attn_flat = attn_tiles.reshape(local_tiles * tile_len, col_width)
    grad_weight = lax.psum_scatter(
        lax.dot_general(
            full_rows, attn_flat, (((0,), (0,)), ((), ())), preferred_element_type=jnp.float32
        ).astype(jnp.bfloat16),
        ("z", "core"),
        scatter_dimension=0,
        tiled=True,
    )
    return (grad_q, grad_k, grad_v, grad_weight)


def solution(mesh):
    ctx_count = mesh.shape["ctx"]
    tp_count = mesh.shape["tp"]
    devices = mesh.devices.reshape(ctx_count // CORES, CORES, tp_count)
    chip_mesh = Mesh(devices, ("z", "core", "tp"))
    tiles = ("z", "core")
    in_specs = (
        P(tiles, None, "tp"),
        P(tiles, None, "tp"),
        P(tiles, None, "tp"),
        P((*tiles, "tp"), None),
        P(None, "tp"),
        P(),
        P(),
        P(),
    )
    out_specs = (
        P(tiles, None, "tp"),
        P(tiles, None, "tp"),
        P(tiles, None, "tp"),
        P(tiles, "tp"),
    )
    return jax.shard_map(
        per_device, mesh=chip_mesh, in_specs=in_specs, out_specs=out_specs, check_vma=False
    )
```

```python
import math

import jax
import jax.numpy as jnp
from jax import lax
from jax.sharding import Mesh
from jax.sharding import PartitionSpec as P

HD = 128
CORES = 2


def slot_tables(nbr_tiles, nbr_valid, slot_of):
    tile_count = slot_of.shape[0]
    slot_index = jnp.arange(tile_count, dtype=jnp.int32)
    matches = (slot_of[:, None] == slot_index[None, :]).astype(jnp.int32)
    near_tiles = jnp.einsum("ts,tj->sj", matches, nbr_tiles)
    live_mask = jnp.einsum("ts,tj->sj", matches, nbr_valid)
    found = (near_tiles[:, :, None] == slot_index[None, None, :]).astype(jnp.int32)
    key_slot = jnp.sum(found * slot_of[None, None, :], axis=2)
    return (key_slot, live_mask)


def to_head(arrays, local_tiles, tile_len, heads_here):
    stacked = jnp.stack(
        [a.reshape(local_tiles, tile_len, heads_here, HD) for a in arrays], axis=1
    )
    moved = lax.all_to_all(stacked, "core", split_axis=3, concat_axis=0, tiled=True)
    return moved.reshape(local_tiles * heads_here, len(arrays), tile_len, HD)


def from_head(arrays, local_tiles, tile_len, heads_here):
    stacked = jnp.stack(arrays, axis=1)[:, :, :, None, :]
    moved = lax.all_to_all(stacked, "core", split_axis=0, concat_axis=3, tiled=True)
    return tuple(
        moved[:, n].reshape(local_tiles, tile_len, heads_here * HD) for n in range(len(arrays))
    )


def ring_gather(x, axis, count):
    ahead = [(i, (i - 1) % count) for i in range(count)]
    behind = [(i, (i + 1) % count) for i in range(count)]
    half = count // 2
    later = [x]
    earlier = []
    down = x
    up = x
    for _ in range(1, half):
        down = lax.ppermute(down, axis, ahead)
        up = lax.ppermute(up, axis, behind)
        later.append(down)
        earlier.append(up)
    if count % 2 == 0 and count > 1:
        cut = x.shape[0] // 2
        first = lax.ppermute(up[:cut], axis, behind)
        second = lax.ppermute(down[cut:], axis, ahead)
        later.append(jnp.concatenate([first, second], axis=0))
    return jnp.concatenate(later + earlier[::-1], axis=0)


def ring_index(slots, own, chip_tiles, count):
    return ((slots // chip_tiles - own) % count) * chip_tiles + slots % chip_tiles


def per_device(q_act, k_act, v_act, grad_out, w_out, nbr_tiles, nbr_valid, slot_of):
    local_tiles, tile_len, col_width = q_act.shape
    heads_here = col_width // HD
    score_scale = 1.0 / math.sqrt(HD)
    chip_tiles = local_tiles * heads_here
    z_count = lax.axis_size("z")
    own_z = lax.axis_index("z")
    first_slot = own_z * chip_tiles
    key_slot, live_mask = slot_tables(nbr_tiles, nbr_valid, slot_of)
    tile_count = key_slot.shape[0]
    list_len = key_slot.shape[1]
    near_slots = lax.dynamic_slice_in_dim(key_slot, first_slot, chip_tiles, 0)
    near_live = lax.dynamic_slice_in_dim(live_mask, first_slot, chip_tiles, 0)

    full_rows = lax.all_gather(grad_out, "tp", axis=0, tiled=True)
    grad_flat = jnp.dot(full_rows, w_out, preferred_element_type=jnp.float32).astype(jnp.bfloat16)
    grad_tiles = grad_flat.reshape(local_tiles, tile_len, col_width)

    head_parts = to_head((k_act, v_act, q_act), local_tiles, tile_len, heads_here)
    key_h = head_parts[:, 0]
    value_h = head_parts[:, 1]
    query_h = head_parts[:, 2]
    grad_h = to_head((grad_tiles,), local_tiles, tile_len, heads_here)[:, 0]

    kv_all = ring_gather(head_parts[:, 0:2], "z", z_count)
    near_index = ring_index(near_slots.reshape(-1), own_z, chip_tiles, z_count)
    near = kv_all[near_index].reshape(chip_tiles, list_len, 2, tile_len, HD)
    near_keys = near[:, :, 0].reshape(chip_tiles, list_len * tile_len, HD)
    near_values = near[:, :, 1].reshape(chip_tiles, list_len * tile_len, HD)
    live_cells = jnp.repeat(near_live > 0, tile_len, axis=1)[:, None, :]

    scores = (
        jnp.einsum("sad,sbd->sab", query_h, near_keys, preferred_element_type=jnp.float32)
        * score_scale
    )
    row_peak = jnp.max(jnp.where(live_cells, scores, -1e30), axis=2, keepdims=True)
    row_total = jnp.sum(
        jnp.where(live_cells, jnp.exp(scores - row_peak), 0.0), axis=2, keepdims=True
    )
    log_total = row_peak + jnp.log(row_total)
    prob_full = jnp.where(live_cells, jnp.exp(scores - log_total), 0.0)
    prob_half = prob_full.astype(jnp.bfloat16)
    attn_h = jnp.einsum(
        "sab,sbd->sad", prob_half, near_values, preferred_element_type=jnp.float32
    ).astype(jnp.bfloat16)
    row_delta = jnp.einsum("sad,sad->sa", grad_h, attn_h, preferred_element_type=jnp.float32)
    grad_prob = jnp.einsum(
        "sad,sbd->sab", grad_h, near_values, preferred_element_type=jnp.float32
    )
    grad_score = (prob_full * (grad_prob - row_delta[:, :, None])).astype(jnp.bfloat16)
    grad_query_h = (
        jnp.einsum("sab,sbd->sad", grad_score, near_keys, preferred_element_type=jnp.float32)
        * score_scale
    ).astype(jnp.bfloat16)

    attn_tiles, grad_q = from_head((attn_h, grad_query_h), local_tiles, tile_len, heads_here)

    qg_all = lax.all_gather(jnp.stack([query_h, grad_h], axis=1), "z", axis=0, tiled=True)
    stats_all = lax.all_gather(
        jnp.stack([log_total[:, :, 0], row_delta], axis=1), "z", axis=0, tiled=True
    )

    owned_slots = first_slot + jnp.arange(chip_tiles, dtype=jnp.int32)
    pair_hits = (key_slot[:, :, None] == owned_slots[None, None, :]) & (live_mask[:, :, None] > 0)
    named_by = jnp.any(pair_hits, axis=1).astype(jnp.int32)
    rank_of = jnp.cumsum(named_by, axis=0) - 1
    list_pos = jnp.arange(list_len, dtype=jnp.int32)
    placed = (named_by[:, :, None] > 0) & (rank_of[:, :, None] == list_pos[None, None, :])
    slot_index = jnp.arange(tile_count, dtype=jnp.int32)
    picked = jnp.sum(placed.astype(jnp.int32) * slot_index[:, None, None], axis=0)
    picked_live = jnp.any(placed, axis=0)

    picked_index = picked.reshape(-1)
    rows = qg_all[picked_index].reshape(chip_tiles, list_len, 2, tile_len, HD)
    query_rows = rows[:, :, 0].reshape(chip_tiles, list_len * tile_len, HD)
    grad_rows = rows[:, :, 1].reshape(chip_tiles, list_len * tile_len, HD)
    stat_rows = stats_all[picked_index].reshape(chip_tiles, list_len, 2, tile_len)
    total_rows = stat_rows[:, :, 0].reshape(chip_tiles, 1, list_len * tile_len)
    delta_rows = stat_rows[:, :, 1].reshape(chip_tiles, 1, list_len * tile_len)
    keep_pair = jnp.repeat(picked_live, tile_len, axis=1)[:, None, :]

    owner_scores = (
        jnp.einsum("tbd,tad->tba", key_h, query_rows, preferred_element_type=jnp.float32)
        * score_scale
    )
    owner_probs = jnp.where(keep_pair, jnp.exp(owner_scores - total_rows), 0.0)
    owner_grad_prob = jnp.einsum(
        "tbd,tad->tba", value_h, grad_rows, preferred_element_type=jnp.float32
    )
    owner_grad_score = (owner_probs * (owner_grad_prob - delta_rows)).astype(jnp.bfloat16)
    grad_key_h = (
        jnp.einsum("tba,tad->tbd", owner_grad_score, query_rows, preferred_element_type=jnp.float32)
        * score_scale
    ).astype(jnp.bfloat16)
    grad_value_h = jnp.einsum(
        "tba,tad->tbd", owner_probs.astype(jnp.bfloat16), grad_rows, preferred_element_type=jnp.float32
    ).astype(jnp.bfloat16)

    grad_k, grad_v = from_head((grad_key_h, grad_value_h), local_tiles, tile_len, heads_here)

    attn_flat = attn_tiles.reshape(local_tiles * tile_len, col_width)
    weight_part = lax.dot_general(
        full_rows, attn_flat, (((0,), (0,)), ((), ())), preferred_element_type=jnp.float32
    )
    model_width = weight_part.shape[0]
    block_rows = model_width // (z_count * CORES)
    by_core = weight_part.reshape(z_count, CORES, block_rows, col_width).transpose(1, 0, 2, 3)
    chip_sum = lax.psum_scatter(by_core, "core", scatter_dimension=0, tiled=True)
    grad_weight = lax.psum_scatter(
        chip_sum.reshape(z_count * block_rows, col_width).astype(jnp.bfloat16),
        "z",
        scatter_dimension=0,
        tiled=True,
    )
    return (grad_q, grad_k, grad_v, grad_weight)


def solution(mesh):
    ctx_count = mesh.shape["ctx"]
    tp_count = mesh.shape["tp"]
    devices = mesh.devices.reshape(ctx_count // CORES, CORES, tp_count)
    chip_mesh = Mesh(devices, ("z", "core", "tp"))
    tiles = ("z", "core")
    in_specs = (
        P(tiles, None, "tp"),
        P(tiles, None, "tp"),
        P(tiles, None, "tp"),
        P((*tiles, "tp"), None),
        P(None, "tp"),
        P(),
        P(),
        P(),
    )
    out_specs = (
        P(tiles, None, "tp"),
        P(tiles, None, "tp"),
        P(tiles, None, "tp"),
        P(tiles, "tp"),
    )
    return jax.shard_map(
        per_device, mesh=chip_mesh, in_specs=in_specs, out_specs=out_specs, check_vma=False
    )
```

```python
import math

import jax
import jax.numpy as jnp
from jax import lax
from jax.sharding import Mesh
from jax.sharding import PartitionSpec as P

HD = 128
CORES = 2


def slot_tables(nbr_tiles, nbr_valid, slot_of):
    tile_count = slot_of.shape[0]
    slot_index = jnp.arange(tile_count, dtype=jnp.int32)
    matches = (slot_of[:, None] == slot_index[None, :]).astype(jnp.int32)
    near_tiles = jnp.einsum("ts,tj->sj", matches, nbr_tiles)
    live_mask = jnp.einsum("ts,tj->sj", matches, nbr_valid)
    found = (near_tiles[:, :, None] == slot_index[None, None, :]).astype(jnp.int32)
    key_slot = jnp.sum(found * slot_of[None, None, :], axis=2)
    return (key_slot, live_mask)


def to_head(arrays, local_tiles, tile_len, heads_here):
    stacked = jnp.stack(
        [a.reshape(local_tiles, tile_len, heads_here, HD) for a in arrays], axis=1
    )
    moved = lax.all_to_all(stacked, "core", split_axis=3, concat_axis=0, tiled=True)
    return moved.reshape(local_tiles * heads_here, len(arrays), tile_len, HD)


def from_head(arrays, local_tiles, tile_len, heads_here):
    stacked = jnp.stack(arrays, axis=1)[:, :, :, None, :]
    moved = lax.all_to_all(stacked, "core", split_axis=0, concat_axis=3, tiled=True)
    return tuple(
        moved[:, n].reshape(local_tiles, tile_len, heads_here * HD) for n in range(len(arrays))
    )


def ring_gather(x, axis, count, hold=None):
    ahead = [(i, (i - 1) % count) for i in range(count)]
    behind = [(i, (i + 1) % count) for i in range(count)]
    half = count // 2
    later = [x]
    earlier = []
    down = x
    up = x
    for _ in range(1, half):
        down = lax.ppermute(down, axis, ahead)
        up = lax.ppermute(up, axis, behind)
        later.append(down)
        earlier.append(up)
    if hold is not None:
        up, down, hold = lax.optimization_barrier((up, down, hold))
    if count % 2 == 0 and count > 1:
        cut = x.shape[0] // 2
        first = lax.ppermute(up[:cut], axis, behind)
        second = lax.ppermute(down[cut:], axis, ahead)
        later.append(jnp.concatenate([first, second], axis=0))
    return jnp.concatenate(later + earlier[::-1], axis=0), hold


def ring_index(slots, own, chip_tiles, count):
    return ((slots // chip_tiles - own) % count) * chip_tiles + slots % chip_tiles


def per_device(q_act, k_act, v_act, grad_out, w_out, nbr_tiles, nbr_valid, slot_of):
    local_tiles, tile_len, col_width = q_act.shape
    heads_here = col_width // HD
    score_scale = 1.0 / math.sqrt(HD)
    chip_tiles = local_tiles * heads_here
    z_count = lax.axis_size("z")
    own_z = lax.axis_index("z")
    first_slot = own_z * chip_tiles
    key_slot, live_mask = slot_tables(nbr_tiles, nbr_valid, slot_of)
    tile_count = key_slot.shape[0]
    list_len = key_slot.shape[1]
    near_slots = lax.dynamic_slice_in_dim(key_slot, first_slot, chip_tiles, 0)
    near_live = lax.dynamic_slice_in_dim(live_mask, first_slot, chip_tiles, 0)

    full_rows = lax.all_gather(grad_out, "tp", axis=0, tiled=True)
    grad_flat = jnp.dot(full_rows, w_out, preferred_element_type=jnp.float32).astype(jnp.bfloat16)
    grad_tiles = grad_flat.reshape(local_tiles, tile_len, col_width)

    head_parts = to_head((k_act, v_act, q_act), local_tiles, tile_len, heads_here)
    key_h = head_parts[:, 0]
    value_h = head_parts[:, 1]
    query_h = head_parts[:, 2]
    grad_h = to_head((grad_tiles,), local_tiles, tile_len, heads_here)[:, 0]

    kv_all, grad_h = ring_gather(head_parts[:, 0:2], "z", z_count, grad_h)
    near_index = ring_index(near_slots.reshape(-1), own_z, chip_tiles, z_count)
    near = kv_all[near_index].reshape(chip_tiles, list_len, 2, tile_len, HD)
    near_keys = near[:, :, 0].reshape(chip_tiles, list_len * tile_len, HD)
    near_values = near[:, :, 1].reshape(chip_tiles, list_len * tile_len, HD)
    live_cells = jnp.repeat(near_live > 0, tile_len, axis=1)[:, None, :]

    scores = (
        jnp.einsum("sad,sbd->sab", query_h, near_keys, preferred_element_type=jnp.float32)
        * score_scale
    )
    row_peak = jnp.max(jnp.where(live_cells, scores, -1e30), axis=2, keepdims=True)
    row_total = jnp.sum(
        jnp.where(live_cells, jnp.exp(scores - row_peak), 0.0), axis=2, keepdims=True
    )
    log_total = row_peak + jnp.log(row_total)
    prob_full = jnp.where(live_cells, jnp.exp(scores - log_total), 0.0)
    prob_half = prob_full.astype(jnp.bfloat16)
    attn_h = jnp.einsum(
        "sab,sbd->sad", prob_half, near_values, preferred_element_type=jnp.float32
    ).astype(jnp.bfloat16)
    row_delta = jnp.einsum("sad,sad->sa", grad_h, attn_h, preferred_element_type=jnp.float32)
    grad_prob = jnp.einsum(
        "sad,sbd->sab", grad_h, near_values, preferred_element_type=jnp.float32
    )
    grad_score = (prob_full * (grad_prob - row_delta[:, :, None])).astype(jnp.bfloat16)
    grad_query_h = (
        jnp.einsum("sab,sbd->sad", grad_score, near_keys, preferred_element_type=jnp.float32)
        * score_scale
    ).astype(jnp.bfloat16)

    attn_tiles, grad_q = from_head((attn_h, grad_query_h), local_tiles, tile_len, heads_here)

    qg_all, _ = ring_gather(jnp.stack([query_h, grad_h], axis=1), "z", z_count)
    stats_all, _ = ring_gather(jnp.stack([log_total[:, :, 0], row_delta], axis=1), "z", z_count)

    owned_slots = first_slot + jnp.arange(chip_tiles, dtype=jnp.int32)
    pair_hits = (key_slot[:, :, None] == owned_slots[None, None, :]) & (live_mask[:, :, None] > 0)
    named_by = jnp.any(pair_hits, axis=1).astype(jnp.int32)
    rank_of = jnp.cumsum(named_by, axis=0) - 1
    list_pos = jnp.arange(list_len, dtype=jnp.int32)
    placed = (named_by[:, :, None] > 0) & (rank_of[:, :, None] == list_pos[None, None, :])
    slot_index = jnp.arange(tile_count, dtype=jnp.int32)
    picked = jnp.sum(placed.astype(jnp.int32) * slot_index[:, None, None], axis=0)
    picked_live = jnp.any(placed, axis=0)

    picked_index = ring_index(picked.reshape(-1), own_z, chip_tiles, z_count)
    rows = qg_all[picked_index].reshape(chip_tiles, list_len, 2, tile_len, HD)
    query_rows = rows[:, :, 0].reshape(chip_tiles, list_len * tile_len, HD)
    grad_rows = rows[:, :, 1].reshape(chip_tiles, list_len * tile_len, HD)
    stat_rows = stats_all[picked_index].reshape(chip_tiles, list_len, 2, tile_len)
    total_rows = stat_rows[:, :, 0].reshape(chip_tiles, 1, list_len * tile_len)
    delta_rows = stat_rows[:, :, 1].reshape(chip_tiles, 1, list_len * tile_len)
    keep_pair = jnp.repeat(picked_live, tile_len, axis=1)[:, None, :]

    owner_scores = (
        jnp.einsum("tbd,tad->tba", key_h, query_rows, preferred_element_type=jnp.float32)
        * score_scale
    )
    owner_probs = jnp.where(keep_pair, jnp.exp(owner_scores - total_rows), 0.0)
    owner_grad_prob = jnp.einsum(
        "tbd,tad->tba", value_h, grad_rows, preferred_element_type=jnp.float32
    )
    owner_grad_score = (owner_probs * (owner_grad_prob - delta_rows)).astype(jnp.bfloat16)
    grad_key_h = (
        jnp.einsum("tba,tad->tbd", owner_grad_score, query_rows, preferred_element_type=jnp.float32)
        * score_scale
    ).astype(jnp.bfloat16)
    grad_value_h = jnp.einsum(
        "tba,tad->tbd", owner_probs.astype(jnp.bfloat16), grad_rows, preferred_element_type=jnp.float32
    ).astype(jnp.bfloat16)

    grad_k, grad_v = from_head((grad_key_h, grad_value_h), local_tiles, tile_len, heads_here)

    attn_flat = attn_tiles.reshape(local_tiles * tile_len, col_width)
    weight_part = lax.dot_general(
        full_rows, attn_flat, (((0,), (0,)), ((), ())), preferred_element_type=jnp.float32
    )
    model_width = weight_part.shape[0]
    block_rows = model_width // (z_count * CORES)
    by_core = weight_part.reshape(z_count, CORES, block_rows, col_width).transpose(1, 0, 2, 3)
    chip_sum = lax.psum_scatter(by_core, "core", scatter_dimension=0, tiled=True)
    grad_weight = lax.psum_scatter(
        chip_sum.reshape(z_count * block_rows, col_width).astype(jnp.bfloat16),
        "z",
        scatter_dimension=0,
        tiled=True,
    )
    return (grad_q, grad_k, grad_v, grad_weight)


def solution(mesh):
    ctx_count = mesh.shape["ctx"]
    tp_count = mesh.shape["tp"]
    devices = mesh.devices.reshape(ctx_count // CORES, CORES, tp_count)
    chip_mesh = Mesh(devices, ("z", "core", "tp"))
    tiles = ("z", "core")
    in_specs = (
        P(tiles, None, "tp"),
        P(tiles, None, "tp"),
        P(tiles, None, "tp"),
        P((*tiles, "tp"), None),
        P(None, "tp"),
        P(),
        P(),
        P(),
    )
    out_specs = (
        P(tiles, None, "tp"),
        P(tiles, None, "tp"),
        P(tiles, None, "tp"),
        P(tiles, "tp"),
    )
    return jax.shard_map(
        per_device, mesh=chip_mesh, in_specs=in_specs, out_specs=out_specs, check_vma=False
    )
```

```python
import math

import jax
import jax.numpy as jnp
from jax import lax
from jax.sharding import Mesh
from jax.sharding import PartitionSpec as P

HD = 128
CORES = 2


def slot_tables(nbr_tiles, nbr_valid, slot_of):
    tile_count = slot_of.shape[0]
    slot_index = jnp.arange(tile_count, dtype=jnp.int32)
    matches = (slot_of[:, None] == slot_index[None, :]).astype(jnp.int32)
    near_tiles = jnp.einsum("ts,tj->sj", matches, nbr_tiles)
    live_mask = jnp.einsum("ts,tj->sj", matches, nbr_valid)
    found = (near_tiles[:, :, None] == slot_index[None, None, :]).astype(jnp.int32)
    key_slot = jnp.sum(found * slot_of[None, None, :], axis=2)
    return (key_slot, live_mask)


def to_head(arrays, local_tiles, tile_len, heads_here):
    stacked = jnp.stack(
        [a.reshape(local_tiles, tile_len, heads_here, HD) for a in arrays], axis=1
    )
    moved = lax.all_to_all(stacked, "core", split_axis=3, concat_axis=0, tiled=True)
    return moved.reshape(local_tiles * heads_here, len(arrays), tile_len, HD)


def from_head(arrays, local_tiles, tile_len, heads_here):
    stacked = jnp.stack(arrays, axis=1)[:, :, :, None, :]
    moved = lax.all_to_all(stacked, "core", split_axis=0, concat_axis=3, tiled=True)
    return tuple(
        moved[:, n].reshape(local_tiles, tile_len, heads_here * HD) for n in range(len(arrays))
    )


def ring_gather(x, axis, count):
    ahead = [(i, (i - 1) % count) for i in range(count)]
    behind = [(i, (i + 1) % count) for i in range(count)]
    half = count // 2
    later = [x]
    earlier = []
    down = x
    up = x
    for _ in range(1, half):
        down = lax.ppermute(down, axis, ahead)
        up = lax.ppermute(up, axis, behind)
        later.append(down)
        earlier.append(up)
    if count % 2 == 0 and count > 1:
        cut = x.shape[0] // 2
        first = lax.ppermute(up[:cut], axis, behind)
        second = lax.ppermute(down[cut:], axis, ahead)
        later.append(jnp.concatenate([first, second], axis=0))
    return jnp.concatenate(later + earlier[::-1], axis=0)


def ring_index(slots, own, chip_tiles, count):
    return ((slots // chip_tiles - own) % count) * chip_tiles + slots % chip_tiles


def per_device(q_act, k_act, v_act, grad_out, w_out, nbr_tiles, nbr_valid, slot_of):
    local_tiles, tile_len, col_width = q_act.shape
    heads_here = col_width // HD
    score_scale = 1.0 / math.sqrt(HD)
    chip_tiles = local_tiles * heads_here
    z_count = lax.axis_size("z")
    own_z = lax.axis_index("z")
    first_slot = own_z * chip_tiles
    key_slot, live_mask = slot_tables(nbr_tiles, nbr_valid, slot_of)
    tile_count = key_slot.shape[0]
    list_len = key_slot.shape[1]
    near_slots = lax.dynamic_slice_in_dim(key_slot, first_slot, chip_tiles, 0)
    near_live = lax.dynamic_slice_in_dim(live_mask, first_slot, chip_tiles, 0)

    full_rows = lax.all_gather(grad_out, "tp", axis=0, tiled=True)
    grad_flat = jnp.dot(full_rows, w_out, preferred_element_type=jnp.float32).astype(jnp.bfloat16)
    grad_tiles = grad_flat.reshape(local_tiles, tile_len, col_width)

    head_parts = to_head((k_act, v_act, q_act), local_tiles, tile_len, heads_here)
    key_h = head_parts[:, 0]
    value_h = head_parts[:, 1]
    query_h = head_parts[:, 2]
    grad_h = to_head((grad_tiles,), local_tiles, tile_len, heads_here)[:, 0]

    kv_all = ring_gather(head_parts[:, 0:2], "z", z_count)
    near_index = ring_index(near_slots.reshape(-1), own_z, chip_tiles, z_count)
    near = kv_all[near_index].reshape(chip_tiles, list_len, 2, tile_len, HD)
    near_keys = near[:, :, 0].reshape(chip_tiles, list_len * tile_len, HD)
    near_values = near[:, :, 1].reshape(chip_tiles, list_len * tile_len, HD)
    live_cells = jnp.repeat(near_live > 0, tile_len, axis=1)[:, None, :]

    scores = (
        jnp.einsum("sad,sbd->sab", query_h, near_keys, preferred_element_type=jnp.float32)
        * score_scale
    )
    row_peak = jnp.max(jnp.where(live_cells, scores, -1e30), axis=2, keepdims=True)
    row_total = jnp.sum(
        jnp.where(live_cells, jnp.exp(scores - row_peak), 0.0), axis=2, keepdims=True
    )
    log_total = row_peak + jnp.log(row_total)
    prob_full = jnp.where(live_cells, jnp.exp(scores - log_total), 0.0)
    prob_half = prob_full.astype(jnp.bfloat16)
    attn_h = jnp.einsum(
        "sab,sbd->sad", prob_half, near_values, preferred_element_type=jnp.float32
    ).astype(jnp.bfloat16)
    row_delta = jnp.einsum("sad,sad->sa", grad_h, attn_h, preferred_element_type=jnp.float32)
    grad_prob = jnp.einsum(
        "sad,sbd->sab", grad_h, near_values, preferred_element_type=jnp.float32
    )
    grad_score = (prob_full * (grad_prob - row_delta[:, :, None])).astype(jnp.bfloat16)
    grad_query_h = (
        jnp.einsum("sab,sbd->sad", grad_score, near_keys, preferred_element_type=jnp.float32)
        * score_scale
    ).astype(jnp.bfloat16)

    attn_tiles, grad_q = from_head((attn_h, grad_query_h), local_tiles, tile_len, heads_here)

    qg_all = ring_gather(jnp.stack([query_h, grad_h], axis=1), "z", z_count)
    stats = jnp.stack([log_total[:, :, 0], row_delta], axis=1)
    stats_all = lax.all_to_all(
        jnp.broadcast_to(stats[None], (z_count,) + stats.shape), "z", 0, 0, tiled=True
    ).reshape((z_count * chip_tiles,) + stats.shape[1:])

    owned_slots = first_slot + jnp.arange(chip_tiles, dtype=jnp.int32)
    pair_hits = (key_slot[:, :, None] == owned_slots[None, None, :]) & (live_mask[:, :, None] > 0)
    named_by = jnp.any(pair_hits, axis=1).astype(jnp.int32)
    rank_of = jnp.cumsum(named_by, axis=0) - 1
    list_pos = jnp.arange(list_len, dtype=jnp.int32)
    placed = (named_by[:, :, None] > 0) & (rank_of[:, :, None] == list_pos[None, None, :])
    slot_index = jnp.arange(tile_count, dtype=jnp.int32)
    picked = jnp.sum(placed.astype(jnp.int32) * slot_index[:, None, None], axis=0)
    picked_live = jnp.any(placed, axis=0)

    picked_index = ring_index(picked.reshape(-1), own_z, chip_tiles, z_count)
    rows = qg_all[picked_index].reshape(chip_tiles, list_len, 2, tile_len, HD)
    query_rows = rows[:, :, 0].reshape(chip_tiles, list_len * tile_len, HD)
    grad_rows = rows[:, :, 1].reshape(chip_tiles, list_len * tile_len, HD)
    stat_rows = stats_all[picked.reshape(-1)].reshape(chip_tiles, list_len, 2, tile_len)
    total_rows = stat_rows[:, :, 0].reshape(chip_tiles, 1, list_len * tile_len)
    delta_rows = stat_rows[:, :, 1].reshape(chip_tiles, 1, list_len * tile_len)
    keep_pair = jnp.repeat(picked_live, tile_len, axis=1)[:, None, :]

    owner_scores = (
        jnp.einsum("tbd,tad->tba", key_h, query_rows, preferred_element_type=jnp.float32)
        * score_scale
    )
    owner_probs = jnp.where(keep_pair, jnp.exp(owner_scores - total_rows), 0.0)
    owner_grad_prob = jnp.einsum(
        "tbd,tad->tba", value_h, grad_rows, preferred_element_type=jnp.float32
    )
    owner_grad_score = (owner_probs * (owner_grad_prob - delta_rows)).astype(jnp.bfloat16)
    grad_key_h = (
        jnp.einsum("tba,tad->tbd", owner_grad_score, query_rows, preferred_element_type=jnp.float32)
        * score_scale
    ).astype(jnp.bfloat16)
    grad_value_h = jnp.einsum(
        "tba,tad->tbd", owner_probs.astype(jnp.bfloat16), grad_rows, preferred_element_type=jnp.float32
    ).astype(jnp.bfloat16)

    grad_k, grad_v = from_head((grad_key_h, grad_value_h), local_tiles, tile_len, heads_here)

    attn_flat = attn_tiles.reshape(local_tiles * tile_len, col_width)
    grad_weight = lax.psum_scatter(
        lax.dot_general(
            full_rows, attn_flat, (((0,), (0,)), ((), ())), preferred_element_type=jnp.float32
        ).astype(jnp.bfloat16),
        ("z", "core"),
        scatter_dimension=0,
        tiled=True,
    )
    return (grad_q, grad_k, grad_v, grad_weight)


def solution(mesh):
    ctx_count = mesh.shape["ctx"]
    tp_count = mesh.shape["tp"]
    devices = mesh.devices.reshape(ctx_count // CORES, CORES, tp_count)
    chip_mesh = Mesh(devices, ("z", "core", "tp"))
    tiles = ("z", "core")
    in_specs = (
        P(tiles, None, "tp"),
        P(tiles, None, "tp"),
        P(tiles, None, "tp"),
        P((*tiles, "tp"), None),
        P(None, "tp"),
        P(),
        P(),
        P(),
    )
    out_specs = (
        P(tiles, None, "tp"),
        P(tiles, None, "tp"),
        P(tiles, None, "tp"),
        P(tiles, "tp"),
    )
    return jax.shard_map(
        per_device, mesh=chip_mesh, in_specs=in_specs, out_specs=out_specs, check_vma=False
    )
```

```python
import math

import jax
import jax.numpy as jnp
from jax import lax
from jax.sharding import Mesh
from jax.sharding import PartitionSpec as P

HD = 128
CORES = 2


def slot_tables(nbr_tiles, nbr_valid, slot_of):
    tile_count = slot_of.shape[0]
    slot_index = jnp.arange(tile_count, dtype=jnp.int32)
    matches = (slot_of[:, None] == slot_index[None, :]).astype(jnp.int32)
    near_tiles = jnp.einsum("ts,tj->sj", matches, nbr_tiles)
    live_mask = jnp.einsum("ts,tj->sj", matches, nbr_valid)
    found = (near_tiles[:, :, None] == slot_index[None, None, :]).astype(jnp.int32)
    key_slot = jnp.sum(found * slot_of[None, None, :], axis=2)
    return (key_slot, live_mask)


def to_head(arrays, local_tiles, tile_len, heads_here):
    stacked = jnp.stack(
        [a.reshape(local_tiles, tile_len, heads_here, HD) for a in arrays], axis=1
    )
    moved = lax.all_to_all(stacked, "core", split_axis=3, concat_axis=0, tiled=True)
    return moved.reshape(local_tiles * heads_here, len(arrays), tile_len, HD)


def from_head(arrays, local_tiles, tile_len, heads_here):
    stacked = jnp.stack(arrays, axis=1)[:, :, :, None, :]
    moved = lax.all_to_all(stacked, "core", split_axis=0, concat_axis=3, tiled=True)
    return tuple(
        moved[:, n].reshape(local_tiles, tile_len, heads_here * HD) for n in range(len(arrays))
    )


def ring_gather(x, axis, count):
    ahead = [(i, (i - 1) % count) for i in range(count)]
    behind = [(i, (i + 1) % count) for i in range(count)]
    half = count // 2
    later = [x]
    earlier = []
    down = x
    up = x
    for _ in range(1, half):
        down = lax.ppermute(down, axis, ahead)
        up = lax.ppermute(up, axis, behind)
        later.append(down)
        earlier.append(up)
    if count % 2 == 0 and count > 1:
        cut = x.shape[0] // 2
        first = lax.ppermute(up[:cut], axis, behind)
        second = lax.ppermute(down[cut:], axis, ahead)
        later.append(jnp.concatenate([first, second], axis=0))
    return jnp.concatenate(later + earlier[::-1], axis=0)


class Ring:
    def __init__(self, x, axis, count):
        self.axis = axis
        self.count = count
        self.ahead = [(i, (i - 1) % count) for i in range(count)]
        self.behind = [(i, (i + 1) % count) for i in range(count)]
        self.later = [x]
        self.earlier = []
        self.down = x
        self.up = x
        self.taken = 0

    def step(self, tie=None):
        self.taken += 1
        if self.taken < self.count // 2:
            down = lax.ppermute(self.down, self.axis, self.ahead)
            up = lax.ppermute(self.up, self.axis, self.behind)
            if tie is not None:
                down, up, tie = lax.optimization_barrier((down, up, tie))
            self.down = down
            self.up = up
            self.later.append(down)
            self.earlier.append(up)
        else:
            cut = self.up.shape[0] // 2
            first = lax.ppermute(self.up[:cut], self.axis, self.behind)
            second = lax.ppermute(self.down[cut:], self.axis, self.ahead)
            if tie is not None:
                first, second, tie = lax.optimization_barrier((first, second, tie))
            self.later.append(jnp.concatenate([first, second], axis=0))
        return tie

    def result(self):
        return jnp.concatenate(self.later + self.earlier[::-1], axis=0)


def ring_index(slots, own, chip_tiles, count):
    return ((slots // chip_tiles - own) % count) * chip_tiles + slots % chip_tiles


def per_device(q_act, k_act, v_act, grad_out, w_out, nbr_tiles, nbr_valid, slot_of):
    local_tiles, tile_len, col_width = q_act.shape
    heads_here = col_width // HD
    score_scale = 1.0 / math.sqrt(HD)
    chip_tiles = local_tiles * heads_here
    z_count = lax.axis_size("z")
    own_z = lax.axis_index("z")
    first_slot = own_z * chip_tiles
    key_slot, live_mask = slot_tables(nbr_tiles, nbr_valid, slot_of)
    tile_count = key_slot.shape[0]
    list_len = key_slot.shape[1]
    near_slots = lax.dynamic_slice_in_dim(key_slot, first_slot, chip_tiles, 0)
    near_live = lax.dynamic_slice_in_dim(live_mask, first_slot, chip_tiles, 0)

    full_rows = lax.all_gather(grad_out, "tp", axis=0, tiled=True)
    grad_flat = jnp.dot(full_rows, w_out, preferred_element_type=jnp.float32).astype(jnp.bfloat16)
    grad_tiles = grad_flat.reshape(local_tiles, tile_len, col_width)

    head_parts = to_head((k_act, v_act, q_act), local_tiles, tile_len, heads_here)
    key_h = head_parts[:, 0]
    value_h = head_parts[:, 1]
    query_h = head_parts[:, 2]
    grad_h = to_head((grad_tiles,), local_tiles, tile_len, heads_here)[:, 0]

    kv_ring = Ring(head_parts[:, 0:2], "z", z_count)
    kv_ring.step()
    kv_ring.step()
    grad_h = kv_ring.step(grad_h)
    kv_ring.step()
    kv_all = kv_ring.result()
    near_index = ring_index(near_slots.reshape(-1), own_z, chip_tiles, z_count)
    near = kv_all[near_index].reshape(chip_tiles, list_len, 2, tile_len, HD)
    near_keys = near[:, :, 0].reshape(chip_tiles, list_len * tile_len, HD)
    near_values = near[:, :, 1].reshape(chip_tiles, list_len * tile_len, HD)
    live_cells = jnp.repeat(near_live > 0, tile_len, axis=1)[:, None, :]
    qg_ring = Ring(jnp.stack([query_h, grad_h], axis=1), "z", z_count)
    near_keys, near_values = qg_ring.step((near_keys, near_values))

    scores = (
        jnp.einsum("sad,sbd->sab", query_h, near_keys, preferred_element_type=jnp.float32)
        * score_scale
    )
    row_peak = jnp.max(jnp.where(live_cells, scores, -1e30), axis=2, keepdims=True)
    row_total = jnp.sum(
        jnp.where(live_cells, jnp.exp(scores - row_peak), 0.0), axis=2, keepdims=True
    )
    log_total = row_peak + jnp.log(row_total)
    prob_full = jnp.where(live_cells, jnp.exp(scores - log_total), 0.0)
    prob_half = prob_full.astype(jnp.bfloat16)
    prob_full, prob_half = qg_ring.step((prob_full, prob_half))
    attn_h = jnp.einsum(
        "sab,sbd->sad", prob_half, near_values, preferred_element_type=jnp.float32
    ).astype(jnp.bfloat16)
    row_delta = jnp.einsum("sad,sad->sa", grad_h, attn_h, preferred_element_type=jnp.float32)
    grad_prob = jnp.einsum(
        "sad,sbd->sab", grad_h, near_values, preferred_element_type=jnp.float32
    )
    grad_score = (prob_full * (grad_prob - row_delta[:, :, None])).astype(jnp.bfloat16)
    grad_score = qg_ring.step(grad_score)
    grad_query_h = (
        jnp.einsum("sab,sbd->sad", grad_score, near_keys, preferred_element_type=jnp.float32)
        * score_scale
    ).astype(jnp.bfloat16)

    grad_query_h = qg_ring.step(grad_query_h)
    attn_tiles, grad_q = from_head((attn_h, grad_query_h), local_tiles, tile_len, heads_here)

    qg_all = qg_ring.result()
    stats = jnp.stack([log_total[:, :, 0], row_delta], axis=1)
    stats_all = lax.all_to_all(
        jnp.broadcast_to(stats[None], (z_count,) + stats.shape), "z", 0, 0, tiled=True
    ).reshape((z_count * chip_tiles,) + stats.shape[1:])

    owned_slots = first_slot + jnp.arange(chip_tiles, dtype=jnp.int32)
    pair_hits = (key_slot[:, :, None] == owned_slots[None, None, :]) & (live_mask[:, :, None] > 0)
    named_by = jnp.any(pair_hits, axis=1).astype(jnp.int32)
    rank_of = jnp.cumsum(named_by, axis=0) - 1
    list_pos = jnp.arange(list_len, dtype=jnp.int32)
    placed = (named_by[:, :, None] > 0) & (rank_of[:, :, None] == list_pos[None, None, :])
    slot_index = jnp.arange(tile_count, dtype=jnp.int32)
    picked = jnp.sum(placed.astype(jnp.int32) * slot_index[:, None, None], axis=0)
    picked_live = jnp.any(placed, axis=0)

    picked_index = ring_index(picked.reshape(-1), own_z, chip_tiles, z_count)
    rows = qg_all[picked_index].reshape(chip_tiles, list_len, 2, tile_len, HD)
    query_rows = rows[:, :, 0].reshape(chip_tiles, list_len * tile_len, HD)
    grad_rows = rows[:, :, 1].reshape(chip_tiles, list_len * tile_len, HD)
    stat_rows = stats_all[picked.reshape(-1)].reshape(chip_tiles, list_len, 2, tile_len)
    total_rows = stat_rows[:, :, 0].reshape(chip_tiles, 1, list_len * tile_len)
    delta_rows = stat_rows[:, :, 1].reshape(chip_tiles, 1, list_len * tile_len)
    keep_pair = jnp.repeat(picked_live, tile_len, axis=1)[:, None, :]

    owner_scores = (
        jnp.einsum("tbd,tad->tba", key_h, query_rows, preferred_element_type=jnp.float32)
        * score_scale
    )
    owner_probs = jnp.where(keep_pair, jnp.exp(owner_scores - total_rows), 0.0)
    owner_grad_prob = jnp.einsum(
        "tbd,tad->tba", value_h, grad_rows, preferred_element_type=jnp.float32
    )
    owner_grad_score = (owner_probs * (owner_grad_prob - delta_rows)).astype(jnp.bfloat16)
    grad_key_h = (
        jnp.einsum("tba,tad->tbd", owner_grad_score, query_rows, preferred_element_type=jnp.float32)
        * score_scale
    ).astype(jnp.bfloat16)
    grad_value_h = jnp.einsum(
        "tba,tad->tbd", owner_probs.astype(jnp.bfloat16), grad_rows, preferred_element_type=jnp.float32
    ).astype(jnp.bfloat16)

    grad_k, grad_v = from_head((grad_key_h, grad_value_h), local_tiles, tile_len, heads_here)

    attn_flat = attn_tiles.reshape(local_tiles * tile_len, col_width)
    grad_weight = lax.psum_scatter(
        lax.dot_general(
            full_rows, attn_flat, (((0,), (0,)), ((), ())), preferred_element_type=jnp.float32
        ).astype(jnp.bfloat16),
        ("z", "core"),
        scatter_dimension=0,
        tiled=True,
    )
    return (grad_q, grad_k, grad_v, grad_weight)


def solution(mesh):
    ctx_count = mesh.shape["ctx"]
    tp_count = mesh.shape["tp"]
    devices = mesh.devices.reshape(ctx_count // CORES, CORES, tp_count)
    chip_mesh = Mesh(devices, ("z", "core", "tp"))
    tiles = ("z", "core")
    in_specs = (
        P(tiles, None, "tp"),
        P(tiles, None, "tp"),
        P(tiles, None, "tp"),
        P((*tiles, "tp"), None),
        P(None, "tp"),
        P(),
        P(),
        P(),
    )
    out_specs = (
        P(tiles, None, "tp"),
        P(tiles, None, "tp"),
        P(tiles, None, "tp"),
        P(tiles, "tp"),
    )
    return jax.shard_map(
        per_device, mesh=chip_mesh, in_specs=in_specs, out_specs=out_specs, check_vma=False
    )
```

```python
import math

import jax
import jax.numpy as jnp
from jax import lax
from jax.sharding import Mesh
from jax.sharding import PartitionSpec as P

HD = 128
CORES = 2


def slot_tables(nbr_tiles, nbr_valid, slot_of):
    tile_count = slot_of.shape[0]
    slot_index = jnp.arange(tile_count, dtype=jnp.int32)
    matches = (slot_of[:, None] == slot_index[None, :]).astype(jnp.int32)
    near_tiles = jnp.einsum("ts,tj->sj", matches, nbr_tiles)
    live_mask = jnp.einsum("ts,tj->sj", matches, nbr_valid)
    found = (near_tiles[:, :, None] == slot_index[None, None, :]).astype(jnp.int32)
    key_slot = jnp.sum(found * slot_of[None, None, :], axis=2)
    return (key_slot, live_mask)


def to_head(arrays, local_tiles, tile_len, heads_here):
    stacked = jnp.stack(
        [a.reshape(local_tiles, tile_len, heads_here, HD) for a in arrays], axis=1
    )
    moved = lax.all_to_all(stacked, "core", split_axis=3, concat_axis=0, tiled=True)
    return moved.reshape(local_tiles * heads_here, len(arrays), tile_len, HD)


def from_head(arrays, local_tiles, tile_len, heads_here):
    stacked = jnp.stack(arrays, axis=1)[:, :, :, None, :]
    moved = lax.all_to_all(stacked, "core", split_axis=0, concat_axis=3, tiled=True)
    return tuple(
        moved[:, n].reshape(local_tiles, tile_len, heads_here * HD) for n in range(len(arrays))
    )


def ring_gather(x, axis, count):
    ahead = [(i, (i - 1) % count) for i in range(count)]
    behind = [(i, (i + 1) % count) for i in range(count)]
    half = count // 2
    later = [x]
    earlier = []
    down = x
    up = x
    for _ in range(1, half):
        down = lax.ppermute(down, axis, ahead)
        up = lax.ppermute(up, axis, behind)
        later.append(down)
        earlier.append(up)
    if count % 2 == 0 and count > 1:
        cut = x.shape[0] // 2
        first = lax.ppermute(up[:cut], axis, behind)
        second = lax.ppermute(down[cut:], axis, ahead)
        later.append(jnp.concatenate([first, second], axis=0))
    return jnp.concatenate(later + earlier[::-1], axis=0)


class Ring:
    def __init__(self, x, axis, count):
        self.axis = axis
        self.count = count
        self.ahead = [(i, (i - 1) % count) for i in range(count)]
        self.behind = [(i, (i + 1) % count) for i in range(count)]
        self.later = [x]
        self.earlier = []
        self.down = x
        self.up = x
        self.taken = 0

    def step(self, tie=None):
        self.taken += 1
        if self.taken < self.count // 2:
            down = lax.ppermute(self.down, self.axis, self.ahead)
            up = lax.ppermute(self.up, self.axis, self.behind)
            if tie is not None:
                down, up, tie = lax.optimization_barrier((down, up, tie))
            self.down = down
            self.up = up
            self.later.append(down)
            self.earlier.append(up)
        else:
            cut = self.up.shape[0] // 2
            first = lax.ppermute(self.up[:cut], self.axis, self.behind)
            second = lax.ppermute(self.down[cut:], self.axis, self.ahead)
            if tie is not None:
                first, second, tie = lax.optimization_barrier((first, second, tie))
            self.later.append(jnp.concatenate([first, second], axis=0))
        return tie

    def result(self):
        return jnp.concatenate(self.later + self.earlier[::-1], axis=0)


def ring_index(slots, own, chip_tiles, count):
    return ((slots // chip_tiles - own) % count) * chip_tiles + slots % chip_tiles


def per_device(q_act, k_act, v_act, grad_out, w_out, nbr_tiles, nbr_valid, slot_of):
    local_tiles, tile_len, col_width = q_act.shape
    heads_here = col_width // HD
    score_scale = 1.0 / math.sqrt(HD)
    chip_tiles = local_tiles * heads_here
    z_count = lax.axis_size("z")
    own_z = lax.axis_index("z")
    first_slot = own_z * chip_tiles
    key_slot, live_mask = slot_tables(nbr_tiles, nbr_valid, slot_of)
    tile_count = key_slot.shape[0]
    list_len = key_slot.shape[1]
    near_slots = lax.dynamic_slice_in_dim(key_slot, first_slot, chip_tiles, 0)
    near_live = lax.dynamic_slice_in_dim(live_mask, first_slot, chip_tiles, 0)

    full_rows = lax.all_gather(grad_out, "tp", axis=0, tiled=True)
    grad_flat = jnp.dot(full_rows, w_out, preferred_element_type=jnp.float32).astype(jnp.bfloat16)
    grad_tiles = grad_flat.reshape(local_tiles, tile_len, col_width)

    head_parts = to_head((k_act, v_act, q_act), local_tiles, tile_len, heads_here)
    key_h = head_parts[:, 0]
    value_h = head_parts[:, 1]
    query_h = head_parts[:, 2]
    grad_h = to_head((grad_tiles,), local_tiles, tile_len, heads_here)[:, 0]

    kv_ring = Ring(head_parts[:, 0:2], "z", z_count)
    for _ in range(z_count // 2):
        kv_ring.step()
    kv_all = kv_ring.result()
    near_index = ring_index(near_slots.reshape(-1), own_z, chip_tiles, z_count)
    near = kv_all[near_index].reshape(chip_tiles, list_len, 2, tile_len, HD)
    near_keys = near[:, :, 0].reshape(chip_tiles, list_len * tile_len, HD)
    near_values = near[:, :, 1].reshape(chip_tiles, list_len * tile_len, HD)
    live_cells = jnp.repeat(near_live > 0, tile_len, axis=1)[:, None, :]
    qg_ring = Ring(jnp.stack([query_h, grad_h], axis=1), "z", z_count)
    near_keys, near_values = qg_ring.step((near_keys, near_values))

    scores = (
        jnp.einsum("sad,sbd->sab", query_h, near_keys, preferred_element_type=jnp.float32)
        * score_scale
    )
    row_peak = jnp.max(jnp.where(live_cells, scores, -1e30), axis=2, keepdims=True)
    row_total = jnp.sum(
        jnp.where(live_cells, jnp.exp(scores - row_peak), 0.0), axis=2, keepdims=True
    )
    log_total = row_peak + jnp.log(row_total)
    prob_full = jnp.where(live_cells, jnp.exp(scores - log_total), 0.0)
    prob_half = prob_full.astype(jnp.bfloat16)
    prob_full, prob_half = qg_ring.step((prob_full, prob_half))
    attn_h = jnp.einsum(
        "sab,sbd->sad", prob_half, near_values, preferred_element_type=jnp.float32
    ).astype(jnp.bfloat16)
    (attn_tiles,) = from_head((attn_h,), local_tiles, tile_len, heads_here)
    row_delta = jnp.einsum("sad,sad->sa", grad_h, attn_h, preferred_element_type=jnp.float32)
    grad_prob = jnp.einsum(
        "sad,sbd->sab", grad_h, near_values, preferred_element_type=jnp.float32
    )
    grad_score = (prob_full * (grad_prob - row_delta[:, :, None])).astype(jnp.bfloat16)
    grad_score = qg_ring.step(grad_score)
    grad_query_h = (
        jnp.einsum("sab,sbd->sad", grad_score, near_keys, preferred_element_type=jnp.float32)
        * score_scale
    ).astype(jnp.bfloat16)

    grad_query_h = qg_ring.step(grad_query_h)

    qg_all = qg_ring.result()
    stats = jnp.stack([log_total[:, :, 0], row_delta], axis=1)
    stats_all = lax.all_to_all(
        jnp.broadcast_to(stats[None], (z_count,) + stats.shape), "z", 0, 0, tiled=True
    ).reshape((z_count * chip_tiles,) + stats.shape[1:])

    owned_slots = first_slot + jnp.arange(chip_tiles, dtype=jnp.int32)
    pair_hits = (key_slot[:, :, None] == owned_slots[None, None, :]) & (live_mask[:, :, None] > 0)
    named_by = jnp.any(pair_hits, axis=1).astype(jnp.int32)
    rank_of = jnp.cumsum(named_by, axis=0) - 1
    list_pos = jnp.arange(list_len, dtype=jnp.int32)
    placed = (named_by[:, :, None] > 0) & (rank_of[:, :, None] == list_pos[None, None, :])
    slot_index = jnp.arange(tile_count, dtype=jnp.int32)
    picked = jnp.sum(placed.astype(jnp.int32) * slot_index[:, None, None], axis=0)
    picked_live = jnp.any(placed, axis=0)

    picked_index = ring_index(picked.reshape(-1), own_z, chip_tiles, z_count)
    rows = qg_all[picked_index].reshape(chip_tiles, list_len, 2, tile_len, HD)
    query_rows = rows[:, :, 0].reshape(chip_tiles, list_len * tile_len, HD)
    grad_rows = rows[:, :, 1].reshape(chip_tiles, list_len * tile_len, HD)
    stat_rows = stats_all[picked.reshape(-1)].reshape(chip_tiles, list_len, 2, tile_len)
    total_rows = stat_rows[:, :, 0].reshape(chip_tiles, 1, list_len * tile_len)
    delta_rows = stat_rows[:, :, 1].reshape(chip_tiles, 1, list_len * tile_len)
    keep_pair = jnp.repeat(picked_live, tile_len, axis=1)[:, None, :]

    owner_scores = (
        jnp.einsum("tbd,tad->tba", key_h, query_rows, preferred_element_type=jnp.float32)
        * score_scale
    )
    owner_probs = jnp.where(keep_pair, jnp.exp(owner_scores - total_rows), 0.0)
    owner_grad_prob = jnp.einsum(
        "tbd,tad->tba", value_h, grad_rows, preferred_element_type=jnp.float32
    )
    owner_grad_score = (owner_probs * (owner_grad_prob - delta_rows)).astype(jnp.bfloat16)
    grad_key_h = (
        jnp.einsum("tba,tad->tbd", owner_grad_score, query_rows, preferred_element_type=jnp.float32)
        * score_scale
    ).astype(jnp.bfloat16)
    grad_value_h = jnp.einsum(
        "tba,tad->tbd", owner_probs.astype(jnp.bfloat16), grad_rows, preferred_element_type=jnp.float32
    ).astype(jnp.bfloat16)

    grad_q, grad_k, grad_v = from_head(
        (grad_query_h, grad_key_h, grad_value_h), local_tiles, tile_len, heads_here
    )

    attn_flat = attn_tiles.reshape(local_tiles * tile_len, col_width)
    grad_weight = lax.psum_scatter(
        lax.dot_general(
            full_rows, attn_flat, (((0,), (0,)), ((), ())), preferred_element_type=jnp.float32
        ).astype(jnp.bfloat16),
        ("z", "core"),
        scatter_dimension=0,
        tiled=True,
    )
    return (grad_q, grad_k, grad_v, grad_weight)


def solution(mesh):
    ctx_count = mesh.shape["ctx"]
    tp_count = mesh.shape["tp"]
    devices = mesh.devices.reshape(ctx_count // CORES, CORES, tp_count)
    chip_mesh = Mesh(devices, ("z", "core", "tp"))
    tiles = ("z", "core")
    in_specs = (
        P(tiles, None, "tp"),
        P(tiles, None, "tp"),
        P(tiles, None, "tp"),
        P((*tiles, "tp"), None),
        P(None, "tp"),
        P(),
        P(),
        P(),
    )
    out_specs = (
        P(tiles, None, "tp"),
        P(tiles, None, "tp"),
        P(tiles, None, "tp"),
        P(tiles, "tp"),
    )
    return jax.shard_map(
        per_device, mesh=chip_mesh, in_specs=in_specs, out_specs=out_specs, check_vma=False
    )
```

```python
import math

import jax
import jax.numpy as jnp
from jax import lax
from jax.sharding import Mesh
from jax.sharding import PartitionSpec as P

HD = 128
CORES = 2


def slot_tables(nbr_tiles, nbr_valid, slot_of):
    tile_count = slot_of.shape[0]
    slot_index = jnp.arange(tile_count, dtype=jnp.int32)
    matches = (slot_of[:, None] == slot_index[None, :]).astype(jnp.int32)
    near_tiles = jnp.einsum("ts,tj->sj", matches, nbr_tiles)
    live_mask = jnp.einsum("ts,tj->sj", matches, nbr_valid)
    found = (near_tiles[:, :, None] == slot_index[None, None, :]).astype(jnp.int32)
    key_slot = jnp.sum(found * slot_of[None, None, :], axis=2)
    return (key_slot, live_mask)


def to_head(arrays, local_tiles, tile_len, heads_here):
    stacked = jnp.stack(
        [a.reshape(local_tiles, tile_len, heads_here, HD) for a in arrays], axis=1
    )
    moved = lax.all_to_all(stacked, "core", split_axis=3, concat_axis=0, tiled=True)
    return moved.reshape(local_tiles * heads_here, len(arrays), tile_len, HD)


def from_head(arrays, local_tiles, tile_len, heads_here):
    stacked = jnp.stack(arrays, axis=1)[:, :, :, None, :]
    moved = lax.all_to_all(stacked, "core", split_axis=0, concat_axis=3, tiled=True)
    return tuple(
        moved[:, n].reshape(local_tiles, tile_len, heads_here * HD) for n in range(len(arrays))
    )


def ring_gather(x, axis, count):
    ahead = [(i, (i - 1) % count) for i in range(count)]
    behind = [(i, (i + 1) % count) for i in range(count)]
    half = count // 2
    m = x.shape[0]
    out = jnp.zeros((count * m,) + x.shape[1:], x.dtype).at[:m].set(x)
    down = x
    up = x
    for step in range(1, half):
        down = lax.ppermute(down, axis, ahead)
        up = lax.ppermute(up, axis, behind)
        out = out.at[step * m : (step + 1) * m].set(down)
        out = out.at[(count - step) * m : (count - step + 1) * m].set(up)
    if count % 2 == 0 and count > 1:
        cut = m // 2
        first = lax.ppermute(up[:cut], axis, behind)
        second = lax.ppermute(down[cut:], axis, ahead)
        out = out.at[half * m : half * m + cut].set(first)
        out = out.at[half * m + cut : (half + 1) * m].set(second)
    return out


def ring_index(slots, own, chip_tiles, count):
    return ((slots // chip_tiles - own) % count) * chip_tiles + slots % chip_tiles


def per_device(q_act, k_act, v_act, grad_out, w_out, nbr_tiles, nbr_valid, slot_of):
    local_tiles, tile_len, col_width = q_act.shape
    heads_here = col_width // HD
    score_scale = 1.0 / math.sqrt(HD)
    chip_tiles = local_tiles * heads_here
    z_count = lax.axis_size("z")
    own_z = lax.axis_index("z")
    first_slot = own_z * chip_tiles
    key_slot, live_mask = slot_tables(nbr_tiles, nbr_valid, slot_of)
    tile_count = key_slot.shape[0]
    list_len = key_slot.shape[1]
    near_slots = lax.dynamic_slice_in_dim(key_slot, first_slot, chip_tiles, 0)
    near_live = lax.dynamic_slice_in_dim(live_mask, first_slot, chip_tiles, 0)

    full_rows = lax.all_gather(grad_out, "tp", axis=0, tiled=True)
    grad_flat = jnp.dot(full_rows, w_out, preferred_element_type=jnp.float32).astype(jnp.bfloat16)
    grad_tiles = grad_flat.reshape(local_tiles, tile_len, col_width)

    head_parts = to_head((k_act, v_act, q_act), local_tiles, tile_len, heads_here)
    key_h = head_parts[:, 0]
    value_h = head_parts[:, 1]
    query_h = head_parts[:, 2]
    grad_h = to_head((grad_tiles,), local_tiles, tile_len, heads_here)[:, 0]

    kv_all = ring_gather(head_parts[:, 0:2], "z", z_count)
    near_index = ring_index(near_slots.reshape(-1), own_z, chip_tiles, z_count)
    near = kv_all[near_index].reshape(chip_tiles, list_len, 2, tile_len, HD)
    near_keys = near[:, :, 0].reshape(chip_tiles, list_len * tile_len, HD)
    near_values = near[:, :, 1].reshape(chip_tiles, list_len * tile_len, HD)
    live_cells = jnp.repeat(near_live > 0, tile_len, axis=1)[:, None, :]

    scores = (
        jnp.einsum("sad,sbd->sab", query_h, near_keys, preferred_element_type=jnp.float32)
        * score_scale
    )
    row_peak = jnp.max(jnp.where(live_cells, scores, -1e30), axis=2, keepdims=True)
    row_total = jnp.sum(
        jnp.where(live_cells, jnp.exp(scores - row_peak), 0.0), axis=2, keepdims=True
    )
    log_total = row_peak + jnp.log(row_total)
    prob_full = jnp.where(live_cells, jnp.exp(scores - log_total), 0.0)
    prob_half = prob_full.astype(jnp.bfloat16)
    attn_h = jnp.einsum(
        "sab,sbd->sad", prob_half, near_values, preferred_element_type=jnp.float32
    ).astype(jnp.bfloat16)
    row_delta = jnp.einsum("sad,sad->sa", grad_h, attn_h, preferred_element_type=jnp.float32)
    grad_prob = jnp.einsum(
        "sad,sbd->sab", grad_h, near_values, preferred_element_type=jnp.float32
    )
    grad_score = (prob_full * (grad_prob - row_delta[:, :, None])).astype(jnp.bfloat16)
    grad_query_h = (
        jnp.einsum("sab,sbd->sad", grad_score, near_keys, preferred_element_type=jnp.float32)
        * score_scale
    ).astype(jnp.bfloat16)

    attn_tiles, grad_q = from_head((attn_h, grad_query_h), local_tiles, tile_len, heads_here)

    qg_all = ring_gather(jnp.stack([query_h, grad_h], axis=1), "z", z_count)
    stats = jnp.stack([log_total[:, :, 0], row_delta], axis=1)
    stats_all = lax.all_to_all(
        jnp.broadcast_to(stats[None], (z_count,) + stats.shape), "z", 0, 0, tiled=True
    ).reshape((z_count * chip_tiles,) + stats.shape[1:])

    owned_slots = first_slot + jnp.arange(chip_tiles, dtype=jnp.int32)
    pair_hits = (key_slot[:, :, None] == owned_slots[None, None, :]) & (live_mask[:, :, None] > 0)
    named_by = jnp.any(pair_hits, axis=1).astype(jnp.int32)
    rank_of = jnp.cumsum(named_by, axis=0) - 1
    list_pos = jnp.arange(list_len, dtype=jnp.int32)
    placed = (named_by[:, :, None] > 0) & (rank_of[:, :, None] == list_pos[None, None, :])
    slot_index = jnp.arange(tile_count, dtype=jnp.int32)
    picked = jnp.sum(placed.astype(jnp.int32) * slot_index[:, None, None], axis=0)
    picked_live = jnp.any(placed, axis=0)

    picked_index = ring_index(picked.reshape(-1), own_z, chip_tiles, z_count)
    rows = qg_all[picked_index].reshape(chip_tiles, list_len, 2, tile_len, HD)
    query_rows = rows[:, :, 0].reshape(chip_tiles, list_len * tile_len, HD)
    grad_rows = rows[:, :, 1].reshape(chip_tiles, list_len * tile_len, HD)
    stat_rows = stats_all[picked.reshape(-1)].reshape(chip_tiles, list_len, 2, tile_len)
    total_rows = stat_rows[:, :, 0].reshape(chip_tiles, 1, list_len * tile_len)
    delta_rows = stat_rows[:, :, 1].reshape(chip_tiles, 1, list_len * tile_len)
    keep_pair = jnp.repeat(picked_live, tile_len, axis=1)[:, None, :]

    owner_scores = (
        jnp.einsum("tbd,tad->tba", key_h, query_rows, preferred_element_type=jnp.float32)
        * score_scale
    )
    owner_probs = jnp.where(keep_pair, jnp.exp(owner_scores - total_rows), 0.0)
    owner_grad_prob = jnp.einsum(
        "tbd,tad->tba", value_h, grad_rows, preferred_element_type=jnp.float32
    )
    owner_grad_score = (owner_probs * (owner_grad_prob - delta_rows)).astype(jnp.bfloat16)
    grad_key_h = (
        jnp.einsum("tba,tad->tbd", owner_grad_score, query_rows, preferred_element_type=jnp.float32)
        * score_scale
    ).astype(jnp.bfloat16)
    grad_value_h = jnp.einsum(
        "tba,tad->tbd", owner_probs.astype(jnp.bfloat16), grad_rows, preferred_element_type=jnp.float32
    ).astype(jnp.bfloat16)

    grad_k, grad_v = from_head((grad_key_h, grad_value_h), local_tiles, tile_len, heads_here)

    attn_flat = attn_tiles.reshape(local_tiles * tile_len, col_width)
    grad_weight = lax.psum_scatter(
        lax.dot_general(
            full_rows, attn_flat, (((0,), (0,)), ((), ())), preferred_element_type=jnp.float32
        ).astype(jnp.bfloat16),
        ("z", "core"),
        scatter_dimension=0,
        tiled=True,
    )
    return (grad_q, grad_k, grad_v, grad_weight)


def solution(mesh):
    ctx_count = mesh.shape["ctx"]
    tp_count = mesh.shape["tp"]
    devices = mesh.devices.reshape(ctx_count // CORES, CORES, tp_count)
    chip_mesh = Mesh(devices, ("z", "core", "tp"))
    tiles = ("z", "core")
    in_specs = (
        P(tiles, None, "tp"),
        P(tiles, None, "tp"),
        P(tiles, None, "tp"),
        P((*tiles, "tp"), None),
        P(None, "tp"),
        P(),
        P(),
        P(),
    )
    out_specs = (
        P(tiles, None, "tp"),
        P(tiles, None, "tp"),
        P(tiles, None, "tp"),
        P(tiles, "tp"),
    )
    return jax.shard_map(
        per_device, mesh=chip_mesh, in_specs=in_specs, out_specs=out_specs, check_vma=False
    )
```

```python
import math

import jax
import jax.numpy as jnp
from jax import lax
from jax.sharding import Mesh
from jax.sharding import PartitionSpec as P

HD = 128
CORES = 2


def slot_tables(nbr_tiles, nbr_valid, slot_of):
    tile_count = slot_of.shape[0]
    slot_index = jnp.arange(tile_count, dtype=jnp.int32)
    matches = (slot_of[:, None] == slot_index[None, :]).astype(jnp.int32)
    near_tiles = jnp.einsum("ts,tj->sj", matches, nbr_tiles)
    live_mask = jnp.einsum("ts,tj->sj", matches, nbr_valid)
    found = (near_tiles[:, :, None] == slot_index[None, None, :]).astype(jnp.int32)
    key_slot = jnp.sum(found * slot_of[None, None, :], axis=2)
    return (key_slot, live_mask)


def to_head(arrays, local_tiles, tile_len, heads_here):
    stacked = jnp.stack(
        [a.reshape(local_tiles, tile_len, heads_here, HD) for a in arrays], axis=1
    )
    moved = lax.all_to_all(stacked, "core", split_axis=3, concat_axis=0, tiled=True)
    return moved.reshape(local_tiles * heads_here, len(arrays), tile_len, HD)


def from_head(arrays, local_tiles, tile_len, heads_here):
    stacked = jnp.stack(arrays, axis=1)[:, :, :, None, :]
    moved = lax.all_to_all(stacked, "core", split_axis=0, concat_axis=3, tiled=True)
    return tuple(
        moved[:, n].reshape(local_tiles, tile_len, heads_here * HD) for n in range(len(arrays))
    )


def ring_gather(x, axis, count):
    ahead = [(i, (i - 1) % count) for i in range(count)]
    behind = [(i, (i + 1) % count) for i in range(count)]
    half = count // 2
    m = x.shape[0]
    out = jnp.zeros((count * m,) + x.shape[1:], x.dtype).at[:m].set(x)
    down = x
    up = x
    for step in range(1, half):
        down = lax.ppermute(down, axis, ahead)
        up = lax.ppermute(up, axis, behind)
        out = out.at[step * m : (step + 1) * m].set(down)
        out = out.at[(count - step) * m : (count - step + 1) * m].set(up)
    if count % 2 == 0 and count > 1:
        cut = m // 2
        first = lax.ppermute(up[:cut], axis, behind)
        second = lax.ppermute(down[cut:], axis, ahead)
        out = out.at[half * m : half * m + cut].set(first)
        out = out.at[half * m + cut : (half + 1) * m].set(second)
    return out


def ring_index(slots, own, chip_tiles, count):
    return ((slots // chip_tiles - own) % count) * chip_tiles + slots % chip_tiles


def per_device(q_act, k_act, v_act, grad_out, w_out, nbr_tiles, nbr_valid, slot_of):
    local_tiles, tile_len, col_width = q_act.shape
    heads_here = col_width // HD
    score_scale = 1.0 / math.sqrt(HD)
    chip_tiles = local_tiles * heads_here
    z_count = lax.axis_size("z")
    own_z = lax.axis_index("z")
    first_slot = own_z * chip_tiles
    key_slot, live_mask = slot_tables(nbr_tiles, nbr_valid, slot_of)
    tile_count = key_slot.shape[0]
    list_len = key_slot.shape[1]
    near_slots = lax.dynamic_slice_in_dim(key_slot, first_slot, chip_tiles, 0)
    near_live = lax.dynamic_slice_in_dim(live_mask, first_slot, chip_tiles, 0)

    full_rows = lax.all_gather(grad_out, "tp", axis=0, tiled=True)
    grad_flat = jnp.dot(full_rows, w_out, preferred_element_type=jnp.float32).astype(jnp.bfloat16)
    grad_tiles = grad_flat.reshape(local_tiles, tile_len, col_width)

    head_parts = to_head((k_act, v_act, q_act), local_tiles, tile_len, heads_here)
    key_h = head_parts[:, 0]
    value_h = head_parts[:, 1]
    query_h = head_parts[:, 2]
    grad_h = to_head((grad_tiles,), local_tiles, tile_len, heads_here)[:, 0]

    kv_all = ring_gather(head_parts[:, 0:2], "z", z_count)
    kv_all, grad_h = lax.optimization_barrier((kv_all, grad_h))
    near_index = ring_index(near_slots.reshape(-1), own_z, chip_tiles, z_count)
    near = kv_all[near_index].reshape(chip_tiles, list_len, 2, tile_len, HD)
    near_keys = near[:, :, 0].reshape(chip_tiles, list_len * tile_len, HD)
    near_values = near[:, :, 1].reshape(chip_tiles, list_len * tile_len, HD)
    live_cells = jnp.repeat(near_live > 0, tile_len, axis=1)[:, None, :]

    scores = (
        jnp.einsum("sad,sbd->sab", query_h, near_keys, preferred_element_type=jnp.float32)
        * score_scale
    )
    row_peak = jnp.max(jnp.where(live_cells, scores, -1e30), axis=2, keepdims=True)
    row_total = jnp.sum(
        jnp.where(live_cells, jnp.exp(scores - row_peak), 0.0), axis=2, keepdims=True
    )
    log_total = row_peak + jnp.log(row_total)
    prob_full = jnp.where(live_cells, jnp.exp(scores - log_total), 0.0)
    prob_half = prob_full.astype(jnp.bfloat16)
    attn_h = jnp.einsum(
        "sab,sbd->sad", prob_half, near_values, preferred_element_type=jnp.float32
    ).astype(jnp.bfloat16)
    (attn_tiles,) = from_head((attn_h,), local_tiles, tile_len, heads_here)
    row_delta = jnp.einsum("sad,sad->sa", grad_h, attn_h, preferred_element_type=jnp.float32)
    grad_prob = jnp.einsum(
        "sad,sbd->sab", grad_h, near_values, preferred_element_type=jnp.float32
    )
    grad_score = (prob_full * (grad_prob - row_delta[:, :, None])).astype(jnp.bfloat16)
    grad_query_h = (
        jnp.einsum("sab,sbd->sad", grad_score, near_keys, preferred_element_type=jnp.float32)
        * score_scale
    ).astype(jnp.bfloat16)


    qg_all = ring_gather(jnp.stack([query_h, grad_h], axis=1), "z", z_count)
    stats = jnp.stack([log_total[:, :, 0], row_delta], axis=1)
    stats_all = lax.all_to_all(
        jnp.broadcast_to(stats[None], (z_count,) + stats.shape), "z", 0, 0, tiled=True
    ).reshape((z_count * chip_tiles,) + stats.shape[1:])

    owned_slots = first_slot + jnp.arange(chip_tiles, dtype=jnp.int32)
    pair_hits = (key_slot[:, :, None] == owned_slots[None, None, :]) & (live_mask[:, :, None] > 0)
    named_by = jnp.any(pair_hits, axis=1).astype(jnp.int32)
    rank_of = jnp.cumsum(named_by, axis=0) - 1
    list_pos = jnp.arange(list_len, dtype=jnp.int32)
    placed = (named_by[:, :, None] > 0) & (rank_of[:, :, None] == list_pos[None, None, :])
    slot_index = jnp.arange(tile_count, dtype=jnp.int32)
    picked = jnp.sum(placed.astype(jnp.int32) * slot_index[:, None, None], axis=0)
    picked_live = jnp.any(placed, axis=0)

    picked_index = ring_index(picked.reshape(-1), own_z, chip_tiles, z_count)
    rows = qg_all[picked_index].reshape(chip_tiles, list_len, 2, tile_len, HD)
    query_rows = rows[:, :, 0].reshape(chip_tiles, list_len * tile_len, HD)
    grad_rows = rows[:, :, 1].reshape(chip_tiles, list_len * tile_len, HD)
    stat_rows = stats_all[picked.reshape(-1)].reshape(chip_tiles, list_len, 2, tile_len)
    total_rows = stat_rows[:, :, 0].reshape(chip_tiles, 1, list_len * tile_len)
    delta_rows = stat_rows[:, :, 1].reshape(chip_tiles, 1, list_len * tile_len)
    keep_pair = jnp.repeat(picked_live, tile_len, axis=1)[:, None, :]

    owner_scores = (
        jnp.einsum("tbd,tad->tba", key_h, query_rows, preferred_element_type=jnp.float32)
        * score_scale
    )
    owner_probs = jnp.where(keep_pair, jnp.exp(owner_scores - total_rows), 0.0)
    owner_grad_prob = jnp.einsum(
        "tbd,tad->tba", value_h, grad_rows, preferred_element_type=jnp.float32
    )
    owner_grad_score = (owner_probs * (owner_grad_prob - delta_rows)).astype(jnp.bfloat16)
    grad_key_h = (
        jnp.einsum("tba,tad->tbd", owner_grad_score, query_rows, preferred_element_type=jnp.float32)
        * score_scale
    ).astype(jnp.bfloat16)
    grad_value_h = jnp.einsum(
        "tba,tad->tbd", owner_probs.astype(jnp.bfloat16), grad_rows, preferred_element_type=jnp.float32
    ).astype(jnp.bfloat16)

    grad_q, grad_k, grad_v = from_head(
        (grad_query_h, grad_key_h, grad_value_h), local_tiles, tile_len, heads_here
    )

    attn_flat = attn_tiles.reshape(local_tiles * tile_len, col_width)
    grad_weight = lax.psum_scatter(
        lax.dot_general(
            full_rows, attn_flat, (((0,), (0,)), ((), ())), preferred_element_type=jnp.float32
        ).astype(jnp.bfloat16),
        ("z", "core"),
        scatter_dimension=0,
        tiled=True,
    )
    return (grad_q, grad_k, grad_v, grad_weight)


def solution(mesh):
    ctx_count = mesh.shape["ctx"]
    tp_count = mesh.shape["tp"]
    devices = mesh.devices.reshape(ctx_count // CORES, CORES, tp_count)
    chip_mesh = Mesh(devices, ("z", "core", "tp"))
    tiles = ("z", "core")
    in_specs = (
        P(tiles, None, "tp"),
        P(tiles, None, "tp"),
        P(tiles, None, "tp"),
        P((*tiles, "tp"), None),
        P(None, "tp"),
        P(),
        P(),
        P(),
    )
    out_specs = (
        P(tiles, None, "tp"),
        P(tiles, None, "tp"),
        P(tiles, None, "tp"),
        P(tiles, "tp"),
    )
    return jax.shard_map(
        per_device, mesh=chip_mesh, in_specs=in_specs, out_specs=out_specs, check_vma=False
    )
```

```python
import math

import jax
import jax.numpy as jnp
from jax import lax
from jax.sharding import Mesh
from jax.sharding import PartitionSpec as P

HD = 128
CORES = 2


def slot_tables(nbr_tiles, nbr_valid, slot_of):
    tile_count = slot_of.shape[0]
    slot_index = jnp.arange(tile_count, dtype=jnp.int32)
    matches = (slot_of[:, None] == slot_index[None, :]).astype(jnp.int32)
    near_tiles = jnp.einsum("ts,tj->sj", matches, nbr_tiles)
    live_mask = jnp.einsum("ts,tj->sj", matches, nbr_valid)
    found = (near_tiles[:, :, None] == slot_index[None, None, :]).astype(jnp.int32)
    key_slot = jnp.sum(found * slot_of[None, None, :], axis=2)
    return (key_slot, live_mask)


def to_head(arrays, local_tiles, tile_len, heads_here):
    stacked = jnp.stack(
        [a.reshape(local_tiles, tile_len, heads_here, HD) for a in arrays], axis=1
    )
    moved = lax.all_to_all(stacked, "core", split_axis=3, concat_axis=0, tiled=True)
    return moved.reshape(local_tiles * heads_here, len(arrays), tile_len, HD)


def from_head(arrays, local_tiles, tile_len, heads_here):
    stacked = jnp.stack(arrays, axis=1)[:, :, :, None, :]
    moved = lax.all_to_all(stacked, "core", split_axis=0, concat_axis=3, tiled=True)
    return tuple(
        moved[:, n].reshape(local_tiles, tile_len, heads_here * HD) for n in range(len(arrays))
    )


def ring_gather(x, axis, count):
    ahead = [(i, (i - 1) % count) for i in range(count)]
    behind = [(i, (i + 1) % count) for i in range(count)]
    half = count // 2
    m = x.shape[0]
    out = jnp.zeros((count * m,) + x.shape[1:], x.dtype).at[:m].set(x)
    down = x
    up = x
    for step in range(1, half):
        down = lax.ppermute(down, axis, ahead)
        up = lax.ppermute(up, axis, behind)
        out = out.at[step * m : (step + 1) * m].set(down)
        out = out.at[(count - step) * m : (count - step + 1) * m].set(up)
    if count % 2 == 0 and count > 1:
        cut = m // 2
        first = lax.ppermute(up[:cut], axis, behind)
        second = lax.ppermute(down[cut:], axis, ahead)
        out = out.at[half * m : half * m + cut].set(first)
        out = out.at[half * m + cut : (half + 1) * m].set(second)
    return out


def ring_index(slots, own, chip_tiles, count):
    return ((slots // chip_tiles - own) % count) * chip_tiles + slots % chip_tiles


def per_device(q_act, k_act, v_act, grad_out, w_out, nbr_tiles, nbr_valid, slot_of):
    local_tiles, tile_len, col_width = q_act.shape
    heads_here = col_width // HD
    score_scale = 1.0 / math.sqrt(HD)
    chip_tiles = local_tiles * heads_here
    z_count = lax.axis_size("z")
    own_z = lax.axis_index("z")
    first_slot = own_z * chip_tiles
    key_slot, live_mask = slot_tables(nbr_tiles, nbr_valid, slot_of)
    tile_count = key_slot.shape[0]
    list_len = key_slot.shape[1]
    near_slots = lax.dynamic_slice_in_dim(key_slot, first_slot, chip_tiles, 0)
    near_live = lax.dynamic_slice_in_dim(live_mask, first_slot, chip_tiles, 0)

    full_rows = lax.all_gather(grad_out, "tp", axis=0, tiled=True)
    grad_flat = jnp.dot(full_rows, w_out, preferred_element_type=jnp.float32).astype(jnp.bfloat16)
    grad_tiles = grad_flat.reshape(local_tiles, tile_len, col_width)

    head_parts = to_head((k_act, v_act, q_act), local_tiles, tile_len, heads_here)
    key_h = head_parts[:, 0]
    value_h = head_parts[:, 1]
    query_h = head_parts[:, 2]
    grad_h = to_head((grad_tiles,), local_tiles, tile_len, heads_here)[:, 0]

    kv_all = ring_gather(head_parts[:, 0:2], "z", z_count)
    kv_all, grad_h = lax.optimization_barrier((kv_all, grad_h))
    near_index = ring_index(near_slots.reshape(-1), own_z, chip_tiles, z_count)
    near = kv_all[near_index].reshape(chip_tiles, list_len, 2, tile_len, HD)
    near_keys = near[:, :, 0].reshape(chip_tiles, list_len * tile_len, HD)
    near_values = near[:, :, 1].reshape(chip_tiles, list_len * tile_len, HD)
    live_cells = jnp.repeat(near_live > 0, tile_len, axis=1)[:, None, :]

    scores = (
        jnp.einsum("sad,sbd->sab", query_h, near_keys, preferred_element_type=jnp.float32)
        * score_scale
    )
    row_peak = jnp.max(jnp.where(live_cells, scores, -1e30), axis=2, keepdims=True)
    row_total = jnp.sum(
        jnp.where(live_cells, jnp.exp(scores - row_peak), 0.0), axis=2, keepdims=True
    )
    log_total = row_peak + jnp.log(row_total)
    prob_full = jnp.where(live_cells, jnp.exp(scores - log_total), 0.0)
    prob_half = prob_full.astype(jnp.bfloat16)
    attn_h = jnp.einsum(
        "sab,sbd->sad", prob_half, near_values, preferred_element_type=jnp.float32
    ).astype(jnp.bfloat16)
    (attn_tiles,) = from_head((attn_h,), local_tiles, tile_len, heads_here)
    row_delta = jnp.einsum("sad,sad->sa", grad_h, attn_h, preferred_element_type=jnp.float32)
    grad_prob = jnp.einsum(
        "sad,sbd->sab", grad_h, near_values, preferred_element_type=jnp.float32
    )
    grad_score = (prob_full * (grad_prob - row_delta[:, :, None])).astype(jnp.bfloat16)
    grad_query_h = (
        jnp.einsum("sab,sbd->sad", grad_score, near_keys, preferred_element_type=jnp.float32)
        * score_scale
    ).astype(jnp.bfloat16)


    qg_all = ring_gather(jnp.stack([query_h, grad_h], axis=1), "z", z_count)
    stats = jnp.stack([log_total[:, :, 0], row_delta], axis=1)
    stats_all = lax.all_to_all(
        jnp.broadcast_to(stats[None], (z_count,) + stats.shape), "z", 0, 0, tiled=True
    ).reshape((z_count * chip_tiles,) + stats.shape[1:])

    owned_slots = first_slot + jnp.arange(chip_tiles, dtype=jnp.int32)
    pair_hits = (key_slot[:, :, None] == owned_slots[None, None, :]) & (live_mask[:, :, None] > 0)
    named_by = jnp.any(pair_hits, axis=1).astype(jnp.int32)
    rank_of = jnp.cumsum(named_by, axis=0) - 1
    list_pos = jnp.arange(list_len, dtype=jnp.int32)
    placed = (named_by[:, :, None] > 0) & (rank_of[:, :, None] == list_pos[None, None, :])
    slot_index = jnp.arange(tile_count, dtype=jnp.int32)
    picked = jnp.sum(placed.astype(jnp.int32) * slot_index[:, None, None], axis=0)
    picked_live = jnp.any(placed, axis=0)

    picked_index = ring_index(picked.reshape(-1), own_z, chip_tiles, z_count)
    rows = qg_all[picked_index].reshape(chip_tiles, list_len, 2, tile_len, HD)
    query_rows = rows[:, :, 0].reshape(chip_tiles, list_len * tile_len, HD)
    grad_rows = rows[:, :, 1].reshape(chip_tiles, list_len * tile_len, HD)
    stat_rows = stats_all[picked.reshape(-1)].reshape(chip_tiles, list_len, 2, tile_len)
    total_rows = stat_rows[:, :, 0].reshape(chip_tiles, 1, list_len * tile_len)
    delta_rows = stat_rows[:, :, 1].reshape(chip_tiles, 1, list_len * tile_len)
    keep_pair = jnp.repeat(picked_live, tile_len, axis=1)[:, None, :]

    owner_scores = (
        jnp.einsum("tbd,tad->tba", key_h, query_rows, preferred_element_type=jnp.float32)
        * score_scale
    )
    owner_probs = jnp.where(keep_pair, jnp.exp(owner_scores - total_rows), 0.0)
    owner_grad_prob = jnp.einsum(
        "tbd,tad->tba", value_h, grad_rows, preferred_element_type=jnp.float32
    )
    owner_grad_score = (owner_probs * (owner_grad_prob - delta_rows)).astype(jnp.bfloat16)
    grad_key_h = (
        jnp.einsum("tba,tad->tbd", owner_grad_score, query_rows, preferred_element_type=jnp.float32)
        * score_scale
    ).astype(jnp.bfloat16)
    grad_value_h = jnp.einsum(
        "tba,tad->tbd", owner_probs.astype(jnp.bfloat16), grad_rows, preferred_element_type=jnp.float32
    ).astype(jnp.bfloat16)

    grad_q, grad_k, grad_v = from_head(
        (grad_query_h, grad_key_h, grad_value_h), local_tiles, tile_len, heads_here
    )

    attn_flat = attn_tiles.reshape(local_tiles * tile_len, col_width)
    weight_part = lax.dot_general(
        full_rows, attn_flat, (((0,), (0,)), ((), ())), preferred_element_type=jnp.float32
    )
    block_rows = weight_part.shape[0] // (z_count * CORES)
    by_core = weight_part.reshape(z_count, CORES, block_rows, col_width).transpose(1, 0, 2, 3)
    chip_sum = jnp.sum(lax.all_to_all(by_core, "core", 0, 0, tiled=True), axis=0)
    grad_weight = lax.psum_scatter(
        chip_sum.reshape(z_count * block_rows, col_width).astype(jnp.bfloat16),
        "z",
        scatter_dimension=0,
        tiled=True,
    )
    return (grad_q, grad_k, grad_v, grad_weight)


def solution(mesh):
    ctx_count = mesh.shape["ctx"]
    tp_count = mesh.shape["tp"]
    devices = mesh.devices.reshape(ctx_count // CORES, CORES, tp_count)
    chip_mesh = Mesh(devices, ("z", "core", "tp"))
    tiles = ("z", "core")
    in_specs = (
        P(tiles, None, "tp"),
        P(tiles, None, "tp"),
        P(tiles, None, "tp"),
        P((*tiles, "tp"), None),
        P(None, "tp"),
        P(),
        P(),
        P(),
    )
    out_specs = (
        P(tiles, None, "tp"),
        P(tiles, None, "tp"),
        P(tiles, None, "tp"),
        P(tiles, "tp"),
    )
    return jax.shard_map(
        per_device, mesh=chip_mesh, in_specs=in_specs, out_specs=out_specs, check_vma=False
    )
```

```python
import math

import jax
import jax.numpy as jnp
from jax import lax
from jax.sharding import Mesh
from jax.sharding import PartitionSpec as P

HD = 128
CORES = 2


def slot_tables(nbr_tiles, nbr_valid, slot_of):
    tile_count = slot_of.shape[0]
    slot_index = jnp.arange(tile_count, dtype=jnp.int32)
    matches = (slot_of[:, None] == slot_index[None, :]).astype(jnp.int32)
    near_tiles = jnp.einsum("ts,tj->sj", matches, nbr_tiles)
    live_mask = jnp.einsum("ts,tj->sj", matches, nbr_valid)
    found = (near_tiles[:, :, None] == slot_index[None, None, :]).astype(jnp.int32)
    key_slot = jnp.sum(found * slot_of[None, None, :], axis=2)
    return (key_slot, live_mask)


def to_head(arrays, local_tiles, tile_len, heads_here):
    stacked = jnp.stack(
        [a.reshape(local_tiles, tile_len, heads_here, HD) for a in arrays], axis=1
    )
    moved = lax.all_to_all(stacked, "core", split_axis=3, concat_axis=0, tiled=True)
    return moved.reshape(local_tiles * heads_here, len(arrays), tile_len, HD)


def from_head(arrays, local_tiles, tile_len, heads_here):
    stacked = jnp.stack(arrays, axis=1)[:, :, :, None, :]
    moved = lax.all_to_all(stacked, "core", split_axis=0, concat_axis=3, tiled=True)
    return tuple(
        moved[:, n].reshape(local_tiles, tile_len, heads_here * HD) for n in range(len(arrays))
    )


def ring_gather(x, axis, count):
    ahead = [(i, (i - 1) % count) for i in range(count)]
    behind = [(i, (i + 1) % count) for i in range(count)]
    half = count // 2
    m = x.shape[0]
    out = jnp.zeros((count * m,) + x.shape[1:], x.dtype).at[:m].set(x)
    down = x
    up = x
    for step in range(1, half):
        down = lax.ppermute(down, axis, ahead)
        up = lax.ppermute(up, axis, behind)
        out = out.at[step * m : (step + 1) * m].set(down)
        out = out.at[(count - step) * m : (count - step + 1) * m].set(up)
    if count % 2 == 0 and count > 1:
        cut = m // 2
        first = lax.ppermute(up[:cut], axis, behind)
        second = lax.ppermute(down[cut:], axis, ahead)
        out = out.at[half * m : half * m + cut].set(first)
        out = out.at[half * m + cut : (half + 1) * m].set(second)
    return out


def ring_index(slots, own, chip_tiles, count):
    return ((slots // chip_tiles - own) % count) * chip_tiles + slots % chip_tiles


def per_device(q_act, k_act, v_act, grad_out, w_out, nbr_tiles, nbr_valid, slot_of):
    local_tiles, tile_len, col_width = q_act.shape
    heads_here = col_width // HD
    score_scale = 1.0 / math.sqrt(HD)
    chip_tiles = local_tiles * heads_here
    z_count = lax.axis_size("z")
    own_z = lax.axis_index("z")
    first_slot = own_z * chip_tiles
    key_slot, live_mask = slot_tables(nbr_tiles, nbr_valid, slot_of)
    tile_count = key_slot.shape[0]
    list_len = key_slot.shape[1]
    near_slots = lax.dynamic_slice_in_dim(key_slot, first_slot, chip_tiles, 0)
    near_live = lax.dynamic_slice_in_dim(live_mask, first_slot, chip_tiles, 0)

    full_rows = lax.all_gather(grad_out, "tp", axis=0, tiled=True)
    grad_flat = jnp.dot(full_rows, w_out, preferred_element_type=jnp.float32).astype(jnp.bfloat16)
    grad_tiles = grad_flat.reshape(local_tiles, tile_len, col_width)

    head_parts = to_head((k_act, v_act), local_tiles, tile_len, heads_here)
    key_h = head_parts[:, 0]
    value_h = head_parts[:, 1]
    query_h = to_head((q_act,), local_tiles, tile_len, heads_here)[:, 0]
    grad_h = to_head((grad_tiles,), local_tiles, tile_len, heads_here)[:, 0]

    kv_all = ring_gather(head_parts[:, 0:2], "z", z_count)
    kv_all, grad_h = lax.optimization_barrier((kv_all, grad_h))
    near_index = ring_index(near_slots.reshape(-1), own_z, chip_tiles, z_count)
    near = kv_all[near_index].reshape(chip_tiles, list_len, 2, tile_len, HD)
    near_keys = near[:, :, 0].reshape(chip_tiles, list_len * tile_len, HD)
    near_values = near[:, :, 1].reshape(chip_tiles, list_len * tile_len, HD)
    live_cells = jnp.repeat(near_live > 0, tile_len, axis=1)[:, None, :]

    scores = (
        jnp.einsum("sad,sbd->sab", query_h, near_keys, preferred_element_type=jnp.float32)
        * score_scale
    )
    row_peak = jnp.max(jnp.where(live_cells, scores, -1e30), axis=2, keepdims=True)
    row_total = jnp.sum(
        jnp.where(live_cells, jnp.exp(scores - row_peak), 0.0), axis=2, keepdims=True
    )
    log_total = row_peak + jnp.log(row_total)
    prob_full = jnp.where(live_cells, jnp.exp(scores - log_total), 0.0)
    prob_half = prob_full.astype(jnp.bfloat16)
    attn_h = jnp.einsum(
        "sab,sbd->sad", prob_half, near_values, preferred_element_type=jnp.float32
    ).astype(jnp.bfloat16)
    (attn_tiles,) = from_head((attn_h,), local_tiles, tile_len, heads_here)
    row_delta = jnp.einsum("sad,sad->sa", grad_h, attn_h, preferred_element_type=jnp.float32)
    grad_prob = jnp.einsum(
        "sad,sbd->sab", grad_h, near_values, preferred_element_type=jnp.float32
    )
    grad_score = (prob_full * (grad_prob - row_delta[:, :, None])).astype(jnp.bfloat16)
    grad_query_h = (
        jnp.einsum("sab,sbd->sad", grad_score, near_keys, preferred_element_type=jnp.float32)
        * score_scale
    ).astype(jnp.bfloat16)


    qg_all = ring_gather(jnp.stack([query_h, grad_h], axis=1), "z", z_count)
    stats = jnp.stack([log_total[:, :, 0], row_delta], axis=1)
    stats_all = lax.all_to_all(
        jnp.broadcast_to(stats[None], (z_count,) + stats.shape), "z", 0, 0, tiled=True
    ).reshape((z_count * chip_tiles,) + stats.shape[1:])

    owned_slots = first_slot + jnp.arange(chip_tiles, dtype=jnp.int32)
    pair_hits = (key_slot[:, :, None] == owned_slots[None, None, :]) & (live_mask[:, :, None] > 0)
    named_by = jnp.any(pair_hits, axis=1).astype(jnp.int32)
    rank_of = jnp.cumsum(named_by, axis=0) - 1
    list_pos = jnp.arange(list_len, dtype=jnp.int32)
    placed = (named_by[:, :, None] > 0) & (rank_of[:, :, None] == list_pos[None, None, :])
    slot_index = jnp.arange(tile_count, dtype=jnp.int32)
    picked = jnp.sum(placed.astype(jnp.int32) * slot_index[:, None, None], axis=0)
    picked_live = jnp.any(placed, axis=0)

    picked_index = ring_index(picked.reshape(-1), own_z, chip_tiles, z_count)
    rows = qg_all[picked_index].reshape(chip_tiles, list_len, 2, tile_len, HD)
    query_rows = rows[:, :, 0].reshape(chip_tiles, list_len * tile_len, HD)
    grad_rows = rows[:, :, 1].reshape(chip_tiles, list_len * tile_len, HD)
    stat_rows = stats_all[picked.reshape(-1)].reshape(chip_tiles, list_len, 2, tile_len)
    total_rows = stat_rows[:, :, 0].reshape(chip_tiles, 1, list_len * tile_len)
    delta_rows = stat_rows[:, :, 1].reshape(chip_tiles, 1, list_len * tile_len)
    keep_pair = jnp.repeat(picked_live, tile_len, axis=1)[:, None, :]

    owner_scores = (
        jnp.einsum("tbd,tad->tba", key_h, query_rows, preferred_element_type=jnp.float32)
        * score_scale
    )
    owner_probs = jnp.where(keep_pair, jnp.exp(owner_scores - total_rows), 0.0)
    owner_grad_prob = jnp.einsum(
        "tbd,tad->tba", value_h, grad_rows, preferred_element_type=jnp.float32
    )
    owner_grad_score = (owner_probs * (owner_grad_prob - delta_rows)).astype(jnp.bfloat16)
    grad_key_h = (
        jnp.einsum("tba,tad->tbd", owner_grad_score, query_rows, preferred_element_type=jnp.float32)
        * score_scale
    ).astype(jnp.bfloat16)
    grad_value_h = jnp.einsum(
        "tba,tad->tbd", owner_probs.astype(jnp.bfloat16), grad_rows, preferred_element_type=jnp.float32
    ).astype(jnp.bfloat16)

    grad_q, grad_k, grad_v = from_head(
        (grad_query_h, grad_key_h, grad_value_h), local_tiles, tile_len, heads_here
    )

    attn_flat = attn_tiles.reshape(local_tiles * tile_len, col_width)
    grad_weight = lax.psum_scatter(
        lax.dot_general(
            full_rows, attn_flat, (((0,), (0,)), ((), ())), preferred_element_type=jnp.float32
        ).astype(jnp.bfloat16),
        ("z", "core"),
        scatter_dimension=0,
        tiled=True,
    )
    return (grad_q, grad_k, grad_v, grad_weight)


def solution(mesh):
    ctx_count = mesh.shape["ctx"]
    tp_count = mesh.shape["tp"]
    devices = mesh.devices.reshape(ctx_count // CORES, CORES, tp_count)
    chip_mesh = Mesh(devices, ("z", "core", "tp"))
    tiles = ("z", "core")
    in_specs = (
        P(tiles, None, "tp"),
        P(tiles, None, "tp"),
        P(tiles, None, "tp"),
        P((*tiles, "tp"), None),
        P(None, "tp"),
        P(),
        P(),
        P(),
    )
    out_specs = (
        P(tiles, None, "tp"),
        P(tiles, None, "tp"),
        P(tiles, None, "tp"),
        P(tiles, "tp"),
    )
    return jax.shard_map(
        per_device, mesh=chip_mesh, in_specs=in_specs, out_specs=out_specs, check_vma=False
    )
```

```python
import math

import jax
import jax.numpy as jnp
from jax import lax
from jax.sharding import Mesh
from jax.sharding import PartitionSpec as P

HD = 128
CORES = 2


def slot_tables(nbr_tiles, nbr_valid, slot_of):
    tile_count = slot_of.shape[0]
    slot_index = jnp.arange(tile_count, dtype=jnp.int32)
    matches = (slot_of[:, None] == slot_index[None, :]).astype(jnp.int32)
    near_tiles = jnp.einsum("ts,tj->sj", matches, nbr_tiles)
    live_mask = jnp.einsum("ts,tj->sj", matches, nbr_valid)
    found = (near_tiles[:, :, None] == slot_index[None, None, :]).astype(jnp.int32)
    key_slot = jnp.sum(found * slot_of[None, None, :], axis=2)
    return (key_slot, live_mask)


def to_head(arrays, local_tiles, tile_len, heads_here):
    stacked = jnp.stack(
        [a.reshape(local_tiles, tile_len, heads_here, HD) for a in arrays], axis=1
    )
    moved = lax.all_to_all(stacked, "core", split_axis=3, concat_axis=0, tiled=True)
    return moved.reshape(local_tiles * heads_here, len(arrays), tile_len, HD)


def from_head(arrays, local_tiles, tile_len, heads_here):
    stacked = jnp.stack(arrays, axis=1)[:, :, :, None, :]
    moved = lax.all_to_all(stacked, "core", split_axis=0, concat_axis=3, tiled=True)
    return tuple(
        moved[:, n].reshape(local_tiles, tile_len, heads_here * HD) for n in range(len(arrays))
    )


def ring_gather(x, axis, count):
    ahead = [(i, (i - 1) % count) for i in range(count)]
    behind = [(i, (i + 1) % count) for i in range(count)]
    half = count // 2
    m = x.shape[0]
    out = jnp.zeros((count * m,) + x.shape[1:], x.dtype).at[:m].set(x)
    down = x
    up = x
    for step in range(1, half):
        down = lax.ppermute(down, axis, ahead)
        up = lax.ppermute(up, axis, behind)
        out = out.at[step * m : (step + 1) * m].set(down)
        out = out.at[(count - step) * m : (count - step + 1) * m].set(up)
    if count % 2 == 0 and count > 1:
        cut = m // 2
        first = lax.ppermute(up[:cut], axis, behind)
        second = lax.ppermute(down[cut:], axis, ahead)
        out = out.at[half * m : half * m + cut].set(first)
        out = out.at[half * m + cut : (half + 1) * m].set(second)
    return out


def ring_index(slots, own, chip_tiles, count):
    return ((slots // chip_tiles - own) % count) * chip_tiles + slots % chip_tiles


def per_device(q_act, k_act, v_act, grad_out, w_out, nbr_tiles, nbr_valid, slot_of):
    local_tiles, tile_len, col_width = q_act.shape
    heads_here = col_width // HD
    score_scale = 1.0 / math.sqrt(HD)
    chip_tiles = local_tiles * heads_here
    z_count = lax.axis_size("z")
    own_z = lax.axis_index("z")
    first_slot = own_z * chip_tiles
    key_slot, live_mask = slot_tables(nbr_tiles, nbr_valid, slot_of)
    tile_count = key_slot.shape[0]
    list_len = key_slot.shape[1]
    near_slots = lax.dynamic_slice_in_dim(key_slot, first_slot, chip_tiles, 0)
    near_live = lax.dynamic_slice_in_dim(live_mask, first_slot, chip_tiles, 0)

    full_rows = lax.all_gather(grad_out, "tp", axis=0, tiled=True)
    grad_flat = jnp.dot(full_rows, w_out, preferred_element_type=jnp.float32).astype(jnp.bfloat16)
    grad_tiles = grad_flat.reshape(local_tiles, tile_len, col_width)

    head_parts = to_head((k_act, v_act, q_act), local_tiles, tile_len, heads_here)
    key_h = head_parts[:, 0]
    value_h = head_parts[:, 1]
    query_h = head_parts[:, 2]
    grad_h = to_head((grad_tiles,), local_tiles, tile_len, heads_here)[:, 0]

    kv_all = ring_gather(head_parts[:, 0:2], "z", z_count)
    kv_all, grad_h = lax.optimization_barrier((kv_all, grad_h))
    near_index = ring_index(near_slots.reshape(-1), own_z, chip_tiles, z_count)
    near = kv_all[near_index].reshape(chip_tiles, list_len, 2, tile_len, HD)
    near_keys = near[:, :, 0].reshape(chip_tiles, list_len * tile_len, HD)
    near_values = near[:, :, 1].reshape(chip_tiles, list_len * tile_len, HD)
    live_cells = jnp.repeat(near_live > 0, tile_len, axis=1)[:, None, :]

    scores = (
        jnp.einsum("sad,sbd->sab", query_h, near_keys, preferred_element_type=jnp.float32)
        * score_scale
    )
    row_peak = jnp.max(jnp.where(live_cells, scores, -1e30), axis=2, keepdims=True)
    row_total = jnp.sum(
        jnp.where(live_cells, jnp.exp(scores - row_peak), 0.0), axis=2, keepdims=True
    )
    log_total = row_peak + jnp.log(row_total)
    prob_full = jnp.where(live_cells, jnp.exp(scores - log_total), 0.0)
    prob_half = prob_full.astype(jnp.bfloat16)
    attn_h = jnp.einsum(
        "sab,sbd->sad", prob_half, near_values, preferred_element_type=jnp.float32
    ).astype(jnp.bfloat16)
    (attn_tiles,) = from_head((attn_h,), local_tiles, tile_len, heads_here)
    row_delta = jnp.einsum("sad,sad->sa", grad_h, attn_h, preferred_element_type=jnp.float32)
    grad_prob = jnp.einsum(
        "sad,sbd->sab", grad_h, near_values, preferred_element_type=jnp.float32
    )
    grad_score = (prob_full * (grad_prob - row_delta[:, :, None])).astype(jnp.bfloat16)
    grad_query_h = (
        jnp.einsum("sab,sbd->sad", grad_score, near_keys, preferred_element_type=jnp.float32)
        * score_scale
    ).astype(jnp.bfloat16)
    (grad_q,) = from_head((grad_query_h,), local_tiles, tile_len, heads_here)

    qg_all = ring_gather(jnp.stack([query_h, grad_h], axis=1), "z", z_count)
    stats = jnp.stack([log_total[:, :, 0], row_delta], axis=1)
    stats_all = lax.all_to_all(
        jnp.broadcast_to(stats[None], (z_count,) + stats.shape), "z", 0, 0, tiled=True
    ).reshape((z_count * chip_tiles,) + stats.shape[1:])

    owned_slots = first_slot + jnp.arange(chip_tiles, dtype=jnp.int32)
    pair_hits = (key_slot[:, :, None] == owned_slots[None, None, :]) & (live_mask[:, :, None] > 0)
    named_by = jnp.any(pair_hits, axis=1).astype(jnp.int32)
    rank_of = jnp.cumsum(named_by, axis=0) - 1
    list_pos = jnp.arange(list_len, dtype=jnp.int32)
    placed = (named_by[:, :, None] > 0) & (rank_of[:, :, None] == list_pos[None, None, :])
    slot_index = jnp.arange(tile_count, dtype=jnp.int32)
    picked = jnp.sum(placed.astype(jnp.int32) * slot_index[:, None, None], axis=0)
    picked_live = jnp.any(placed, axis=0)

    picked_index = ring_index(picked.reshape(-1), own_z, chip_tiles, z_count)
    rows = qg_all[picked_index].reshape(chip_tiles, list_len, 2, tile_len, HD)
    query_rows = rows[:, :, 0].reshape(chip_tiles, list_len * tile_len, HD)
    grad_rows = rows[:, :, 1].reshape(chip_tiles, list_len * tile_len, HD)
    stat_rows = stats_all[picked.reshape(-1)].reshape(chip_tiles, list_len, 2, tile_len)
    total_rows = stat_rows[:, :, 0].reshape(chip_tiles, 1, list_len * tile_len)
    delta_rows = stat_rows[:, :, 1].reshape(chip_tiles, 1, list_len * tile_len)
    keep_pair = jnp.repeat(picked_live, tile_len, axis=1)[:, None, :]

    owner_scores = (
        jnp.einsum("tbd,tad->tba", key_h, query_rows, preferred_element_type=jnp.float32)
        * score_scale
    )
    owner_probs = jnp.where(keep_pair, jnp.exp(owner_scores - total_rows), 0.0)
    owner_grad_prob = jnp.einsum(
        "tbd,tad->tba", value_h, grad_rows, preferred_element_type=jnp.float32
    )
    owner_grad_score = (owner_probs * (owner_grad_prob - delta_rows)).astype(jnp.bfloat16)
    grad_key_h = (
        jnp.einsum("tba,tad->tbd", owner_grad_score, query_rows, preferred_element_type=jnp.float32)
        * score_scale
    ).astype(jnp.bfloat16)
    grad_value_h = jnp.einsum(
        "tba,tad->tbd", owner_probs.astype(jnp.bfloat16), grad_rows, preferred_element_type=jnp.float32
    ).astype(jnp.bfloat16)

    grad_k, grad_v = from_head((grad_key_h, grad_value_h), local_tiles, tile_len, heads_here)

    attn_flat = attn_tiles.reshape(local_tiles * tile_len, col_width)
    grad_weight = lax.psum_scatter(
        lax.dot_general(
            full_rows, attn_flat, (((0,), (0,)), ((), ())), preferred_element_type=jnp.float32
        ).astype(jnp.bfloat16),
        ("z", "core"),
        scatter_dimension=0,
        tiled=True,
    )
    return (grad_q, grad_k, grad_v, grad_weight)


def solution(mesh):
    ctx_count = mesh.shape["ctx"]
    tp_count = mesh.shape["tp"]
    devices = mesh.devices.reshape(ctx_count // CORES, CORES, tp_count)
    chip_mesh = Mesh(devices, ("z", "core", "tp"))
    tiles = ("z", "core")
    in_specs = (
        P(tiles, None, "tp"),
        P(tiles, None, "tp"),
        P(tiles, None, "tp"),
        P((*tiles, "tp"), None),
        P(None, "tp"),
        P(),
        P(),
        P(),
    )
    out_specs = (
        P(tiles, None, "tp"),
        P(tiles, None, "tp"),
        P(tiles, None, "tp"),
        P(tiles, "tp"),
    )
    return jax.shard_map(
        per_device, mesh=chip_mesh, in_specs=in_specs, out_specs=out_specs, check_vma=False
    )
```

```python
import math

import jax
import jax.numpy as jnp
from jax import lax
from jax.sharding import Mesh
from jax.sharding import PartitionSpec as P

HD = 128
CORES = 2


def slot_tables(nbr_tiles, nbr_valid, slot_of):
    tile_count = slot_of.shape[0]
    slot_index = jnp.arange(tile_count, dtype=jnp.int32)
    matches = (slot_of[:, None] == slot_index[None, :]).astype(jnp.int32)
    near_tiles = jnp.einsum("ts,tj->sj", matches, nbr_tiles)
    live_mask = jnp.einsum("ts,tj->sj", matches, nbr_valid)
    found = (near_tiles[:, :, None] == slot_index[None, None, :]).astype(jnp.int32)
    key_slot = jnp.sum(found * slot_of[None, None, :], axis=2)
    return (key_slot, live_mask)


def to_head(arrays, local_tiles, tile_len, heads_here):
    stacked = jnp.stack(
        [a.reshape(local_tiles, tile_len, heads_here, HD) for a in arrays], axis=1
    )
    moved = lax.all_to_all(stacked, "core", split_axis=3, concat_axis=0, tiled=True)
    return moved.reshape(local_tiles * heads_here, len(arrays), tile_len, HD)


def from_head(arrays, local_tiles, tile_len, heads_here):
    stacked = jnp.stack(arrays, axis=1)[:, :, :, None, :]
    moved = lax.all_to_all(stacked, "core", split_axis=0, concat_axis=3, tiled=True)
    return tuple(
        moved[:, n].reshape(local_tiles, tile_len, heads_here * HD) for n in range(len(arrays))
    )


def ring_gather(x, axis, count):
    ahead = [(i, (i - 1) % count) for i in range(count)]
    behind = [(i, (i + 1) % count) for i in range(count)]
    half = count // 2
    m = x.shape[0]
    out = jnp.zeros((count * m,) + x.shape[1:], x.dtype).at[:m].set(x)
    down = x
    up = x
    for step in range(1, half):
        down = lax.ppermute(down, axis, ahead)
        up = lax.ppermute(up, axis, behind)
        out = out.at[step * m : (step + 1) * m].set(down)
        out = out.at[(count - step) * m : (count - step + 1) * m].set(up)
    if count % 2 == 0 and count > 1:
        cut = m // 2
        first = lax.ppermute(up[:cut], axis, behind)
        second = lax.ppermute(down[cut:], axis, ahead)
        out = out.at[half * m : half * m + cut].set(first)
        out = out.at[half * m + cut : (half + 1) * m].set(second)
    return out


def ring_index(slots, own, chip_tiles, count):
    return ((slots // chip_tiles - own) % count) * chip_tiles + slots % chip_tiles


def per_device(q_act, k_act, v_act, grad_out, w_out, nbr_tiles, nbr_valid, slot_of):
    local_tiles, tile_len, col_width = q_act.shape
    heads_here = col_width // HD
    score_scale = 1.0 / math.sqrt(HD)
    chip_tiles = local_tiles * heads_here
    z_count = lax.axis_size("z")
    own_z = lax.axis_index("z")
    first_slot = own_z * chip_tiles
    key_slot, live_mask = slot_tables(nbr_tiles, nbr_valid, slot_of)
    tile_count = key_slot.shape[0]
    list_len = key_slot.shape[1]
    near_slots = lax.dynamic_slice_in_dim(key_slot, first_slot, chip_tiles, 0)
    near_live = lax.dynamic_slice_in_dim(live_mask, first_slot, chip_tiles, 0)

    full_rows = lax.all_gather(grad_out, "tp", axis=0, tiled=True)
    grad_flat = jnp.dot(full_rows, w_out, preferred_element_type=jnp.float32).astype(jnp.bfloat16)
    grad_tiles = grad_flat.reshape(local_tiles, tile_len, col_width)

    head_parts = to_head((k_act, v_act, q_act), local_tiles, tile_len, heads_here)
    key_h = head_parts[:, 0]
    value_h = head_parts[:, 1]
    query_h = head_parts[:, 2]
    grad_h = to_head((grad_tiles,), local_tiles, tile_len, heads_here)[:, 0]

    kv_all = ring_gather(head_parts[:, 0:2], "z", z_count)
    kv_all, grad_h = lax.optimization_barrier((kv_all, grad_h))
    near_index = ring_index(near_slots.reshape(-1), own_z, chip_tiles, z_count)
    near = kv_all[near_index].reshape(chip_tiles, list_len, 2, tile_len, HD)
    near_keys = near[:, :, 0].reshape(chip_tiles, list_len * tile_len, HD)
    near_values = near[:, :, 1].reshape(chip_tiles, list_len * tile_len, HD)
    live_cells = jnp.repeat(near_live > 0, tile_len, axis=1)[:, None, :]

    scores = (
        jnp.einsum("sad,sbd->sab", query_h, near_keys, preferred_element_type=jnp.float32)
        * score_scale
    )
    row_peak = jnp.max(jnp.where(live_cells, scores, -1e30), axis=2, keepdims=True)
    row_total = jnp.sum(
        jnp.where(live_cells, jnp.exp(scores - row_peak), 0.0), axis=2, keepdims=True
    )
    log_total = row_peak + jnp.log(row_total)
    prob_full = jnp.where(live_cells, jnp.exp(scores - log_total), 0.0)
    prob_half = prob_full.astype(jnp.bfloat16)
    attn_h = jnp.einsum(
        "sab,sbd->sad", prob_half, near_values, preferred_element_type=jnp.float32
    ).astype(jnp.bfloat16)
    (attn_tiles,) = from_head((attn_h,), local_tiles, tile_len, heads_here)
    row_delta = jnp.einsum("sad,sad->sa", grad_h, attn_h, preferred_element_type=jnp.float32)
    grad_prob = jnp.einsum(
        "sad,sbd->sab", grad_h, near_values, preferred_element_type=jnp.float32
    )
    grad_score = (prob_full * (grad_prob - row_delta[:, :, None])).astype(jnp.bfloat16)
    grad_query_h = (
        jnp.einsum("sab,sbd->sad", grad_score, near_keys, preferred_element_type=jnp.float32)
        * score_scale
    ).astype(jnp.bfloat16)


    qg_all = ring_gather(jnp.stack([query_h, grad_h], axis=1), "z", z_count)
    stats = jnp.stack([log_total[:, :, 0], row_delta], axis=1)
    stats_all = lax.all_to_all(
        jnp.broadcast_to(stats[None], (z_count,) + stats.shape), "z", 0, 0, tiled=True
    ).reshape((z_count * chip_tiles,) + stats.shape[1:])

    owned_slots = first_slot + jnp.arange(chip_tiles, dtype=jnp.int32)
    pair_hits = (key_slot[:, :, None] == owned_slots[None, None, :]) & (live_mask[:, :, None] > 0)
    named_by = jnp.any(pair_hits, axis=1).astype(jnp.int32)
    rank_of = jnp.cumsum(named_by, axis=0) - 1
    list_pos = jnp.arange(list_len, dtype=jnp.int32)
    placed = (named_by[:, :, None] > 0) & (rank_of[:, :, None] == list_pos[None, None, :])
    slot_index = jnp.arange(tile_count, dtype=jnp.int32)
    picked = jnp.sum(placed.astype(jnp.int32) * slot_index[:, None, None], axis=0)
    picked_live = jnp.any(placed, axis=0)

    picked_index = ring_index(picked.reshape(-1), own_z, chip_tiles, z_count)
    rows = qg_all[picked_index].reshape(chip_tiles, list_len, 2, tile_len, HD)
    query_rows = rows[:, :, 0].reshape(chip_tiles, list_len * tile_len, HD)
    grad_rows = rows[:, :, 1].reshape(chip_tiles, list_len * tile_len, HD)
    stat_rows = stats_all[picked.reshape(-1)].reshape(chip_tiles, list_len, 2, tile_len)
    total_rows = stat_rows[:, :, 0].reshape(chip_tiles, 1, list_len * tile_len)
    delta_rows = stat_rows[:, :, 1].reshape(chip_tiles, 1, list_len * tile_len)
    keep_pair = jnp.repeat(picked_live, tile_len, axis=1)[:, None, :]

    owner_scores = (
        jnp.einsum("tbd,tad->tba", key_h, query_rows, preferred_element_type=jnp.float32)
        * score_scale
    )
    owner_probs = jnp.where(keep_pair, jnp.exp(owner_scores - total_rows), 0.0)
    owner_grad_prob = jnp.einsum(
        "tbd,tad->tba", value_h, grad_rows, preferred_element_type=jnp.float32
    )
    owner_grad_score = (owner_probs * (owner_grad_prob - delta_rows)).astype(jnp.bfloat16)
    grad_key_h = (
        jnp.einsum("tba,tad->tbd", owner_grad_score, query_rows, preferred_element_type=jnp.float32)
        * score_scale
    ).astype(jnp.bfloat16)
    grad_value_h = jnp.einsum(
        "tba,tad->tbd", owner_probs.astype(jnp.bfloat16), grad_rows, preferred_element_type=jnp.float32
    ).astype(jnp.bfloat16)

    grad_q, grad_k, grad_v = from_head(
        (grad_query_h, grad_key_h, grad_value_h), local_tiles, tile_len, heads_here
    )

    attn_flat = attn_tiles.reshape(local_tiles * tile_len, col_width)
    token_count, model_width = full_rows.shape
    block_rows = model_width // (z_count * CORES)
    rows_by_core = (
        full_rows.reshape(token_count, z_count, CORES, block_rows)
        .transpose(0, 2, 1, 3)
        .reshape(token_count, model_width)
    )
    weight_part = lax.dot_general(
        rows_by_core, attn_flat, (((0,), (0,)), ((), ())), preferred_element_type=jnp.float32
    )
    chip_sum = lax.psum_scatter(weight_part, "core", scatter_dimension=0, tiled=True)
    grad_weight = lax.psum_scatter(
        chip_sum.astype(jnp.bfloat16), "z", scatter_dimension=0, tiled=True
    )
    return (grad_q, grad_k, grad_v, grad_weight)


def solution(mesh):
    ctx_count = mesh.shape["ctx"]
    tp_count = mesh.shape["tp"]
    devices = mesh.devices.reshape(ctx_count // CORES, CORES, tp_count)
    chip_mesh = Mesh(devices, ("z", "core", "tp"))
    tiles = ("z", "core")
    in_specs = (
        P(tiles, None, "tp"),
        P(tiles, None, "tp"),
        P(tiles, None, "tp"),
        P((*tiles, "tp"), None),
        P(None, "tp"),
        P(),
        P(),
        P(),
    )
    out_specs = (
        P(tiles, None, "tp"),
        P(tiles, None, "tp"),
        P(tiles, None, "tp"),
        P(tiles, "tp"),
    )
    return jax.shard_map(
        per_device, mesh=chip_mesh, in_specs=in_specs, out_specs=out_specs, check_vma=False
    )
```
